32 devices in a mesh: chain: 8 (over z, x), grp: 4 (over y, core).
Axes of the slice: x: 2, y: 2, z: 4, core: 2. Of those that a mesh axis runs over, the one named last changes fastest.
Arguments:
- right_side: float32 [16, 4, 64, 128], P('chain', 'grp'), may hold values from -0.8 to 0.8
- factor: float32 [16, 4, 2, 128, 128], P('chain', 'grp'), may hold values from -1 to 1
- inverse_diag: float32 [16, 4, 128, 128], P('chain', 'grp'), as said below
- pattern: int32 [16, 4, 2], P('chain'), may hold values from 0 to 3, as said below
Outputs:
- forward_result: float32 [16, 4, 64, 128], P('chain', 'grp')
- solution: float32 [16, 4, 64, 128], P('chain', 'grp')
The draws below stay inside these ranges and needn't reach their ends.
Inputs may be any that keep to these rules, and one draw needn't show every extreme that they name: `pattern`: the 2 entries of one supernode are different supernodes of the previous level. `inverse_diag`: every block is lower triangular with a diagonal between 0.75 and 1.05.
All inputs are finite; a program needn't handle non-finite values.
Results may differ from the reference program's by a relative error of at most 0.0002.
Values sent between devices are 32-bit elements; how exact they have to be, the bound alone decides.
No kernel may reach another device: no remote copies, remote signals or barrier semaphores. Data moves between devices by JAX's collectives and lax.ppermute only.
A program may use at most 320 MiB of HBM per device.

```python
import math
import jax
import jax.numpy as jnp
from jax import lax

SUP = 128
SAMPLES = 64
KNB = 2
GROUPS = 4
LEVELS = 16


def draw_inverse_diag(key, part):
    key_lower, key_diag = jax.random.split(key)
    strict_lower = jax.random.normal(key_lower, (LEVELS, GROUPS, SUP, SUP), jnp.float32) * (0.3 / math.sqrt(SUP))
    strict_lower = jnp.tril(strict_lower, -1)
    diagonal = jax.random.uniform(key_diag, (LEVELS, GROUPS, SUP), jnp.float32, 0.75, 1.05)
    return strict_lower + diagonal[..., None] * jnp.eye(SUP, dtype=jnp.float32)


def draw_factor(key, part):
    spread = math.sqrt(0.99 / (0.8625 * KNB * SUP))
    shape = (LEVELS, GROUPS, KNB, SUP, SUP)
    values = jnp.clip(jax.random.normal(key, shape, jnp.float32), -6.0, 6.0) * spread
    return values


def permute_one(subkey):
    return jax.random.permutation(subkey, GROUPS)


def draw_pattern(key, part):
    subkeys = jax.random.split(key, LEVELS * GROUPS)
    orders = jax.vmap(permute_one)(subkeys)
    return orders[:, :KNB].reshape(LEVELS, GROUPS, KNB).astype(jnp.int32)


def level_of(key, shape, shards, least, high):
    level = 1.0
    for position, blocks in shards:
        steps = jax.random.uniform(jax.random.fold_in(jax.random.fold_in(key, 6), position), (blocks,), jnp.float32, least / len(shards), high / len(shards))
        level = level * jnp.repeat(jnp.exp(steps), shape[position] // blocks).reshape((-1,) + (1,) * (len(shape) - 1 - position))
    return level


def gaussian(stream_key, shape, scale, bound, pieces=(), kind=jnp.bfloat16):
    result = jax.random.normal(stream_key, shape, jnp.float32) * scale
    if len(pieces) > 0:
        result = level_of(stream_key, shape, pieces, -0.22, 0.18) * result
    return jnp.clip(result, min=-bound, max=bound).astype(kind)


def setup_inputs(seed: int = 0) -> dict:
    key_list = jax.random.split(jax.random.key(seed), 5)
    right_side = gaussian(key_list[0], (LEVELS, GROUPS, SAMPLES, SUP), 0.1, 0.8, ((0, 8), (1, 4)), jnp.float32)
    factor = draw_factor(jax.random.fold_in(key_list[4], 71), 0)
    inverse_diag = draw_inverse_diag(jax.random.fold_in(key_list[4], 71), 0)
    pattern = draw_pattern(jax.random.fold_in(key_list[4], 71), 0)
    return {"right_side": right_side, "factor": factor, "inverse_diag": inverse_diag, "pattern": pattern}


PRECISE = lax.Precision.HIGHEST


def reference(right_side, factor, inverse_diag, pattern):
    groups = right_side.shape[1]
    onehot = (pattern[..., None] == jnp.arange(groups, dtype=jnp.int32)).astype(jnp.float32)

    def forward_step(previous, inputs):
        source, blocks, inverse, chosen = inputs
        gathered = jnp.einsum("gkh,hsj->gksj", chosen, previous, precision=PRECISE)
        update = jnp.einsum("gksj,gkij->gsi", gathered, blocks, precision=PRECISE)
        updated = jnp.einsum("gsi,gti->gst", source - update, inverse, precision=PRECISE)
        return updated, updated

    zero_state = jnp.zeros(right_side.shape[1:], jnp.float32)
    _, forward_result = lax.scan(forward_step, zero_state, (right_side, factor, inverse_diag, onehot))

    def backward_step(pending, inputs):
        forward_rows, blocks, inverse, chosen = inputs
        answer = jnp.einsum("gsj,gjt->gst", forward_rows - pending, inverse, precision=PRECISE)
        spread = jnp.einsum("gsi,gkij->gksj", answer, blocks, precision=PRECISE)
        passed = jnp.einsum("gkh,gksj->hsj", chosen, spread, precision=PRECISE)
        return passed, answer

    _, solution = lax.scan(backward_step, zero_state, (forward_result, factor, inverse_diag, onehot), reverse=True)
    return forward_result, solution
```

```python
import jax
import jax.numpy as jnp
from jax import lax
from jax.sharding import PartitionSpec as P

PRECISE = lax.Precision.HIGHEST


def matmul(left_side, right_factor):
    return jnp.dot(left_side, right_factor, precision=PRECISE, preferred_element_type=jnp.float32)


def matmul_trans(left_side, right_factor):
    return lax.dot_general(
        left_side,
        right_factor,
        (((1,), (1,)), ((), ())),
        precision=PRECISE,
        preferred_element_type=jnp.float32,
    )


def shards(right_side, factor, inverse_diag, pattern):
    levels = right_side.shape[0]
    samples = right_side.shape[2]
    sup_rows = right_side.shape[3]
    groups = lax.axis_size("grp")
    chain = lax.axis_size("chain")
    level_rows = groups * sup_rows
    my_group = lax.axis_index("grp")
    scaled = jnp.einsum(
        "lgti,lgkij->lgktj",
        inverse_diag,
        factor,
        precision=PRECISE,
        preferred_element_type=jnp.float32,
    )
    lifted = jnp.einsum(
        "lgsi,lgti->lgst",
        right_side,
        inverse_diag,
        precision=PRECISE,
        preferred_element_type=jnp.float32,
    )
    blocks, offsets = (
        lax.all_gather(scaled, "grp", axis=1, tiled=True),
        lax.all_gather(lifted, "grp", axis=1, tiled=True),
    )
    onehot = (pattern[..., None] == jnp.arange(groups, dtype=jnp.int32)).astype(jnp.float32)
    level_maps = -jnp.einsum(
        "lgkh,lgktj->lhjgt", onehot, blocks, precision=PRECISE, preferred_element_type=jnp.float32
    )
    level_maps = level_maps.reshape(levels, level_rows, level_rows)
    sources = offsets.transpose(0, 2, 1, 3).reshape(levels, samples, level_rows)

    def forward_levels(state):
        rows = []
        for level in range(levels):
            state = matmul(state, level_maps[level]) + sources[level]
            rows.append(state)
        return rows

    ahead = [(position, position + 1) for position in range(chain - 1)]
    behind = [(position + 1, position) for position in range(chain - 1)]

    def forward_hop(_, state):
        return lax.ppermute(forward_levels(state)[-1], "chain", ahead)

    incoming = jnp.zeros((samples, level_rows), jnp.float32)
    incoming = lax.fori_loop(0, chain - 1, forward_hop, incoming)
    solved = forward_levels(incoming)

    def backward_levels(running):
        rows = [None] * levels
        for level in reversed(range(levels)):
            rows[level] = solved[level] - running
            running = matmul_trans(-rows[level], level_maps[level])
        return rows, running

    def backward_hop(_, running):
        return lax.ppermute(backward_levels(running)[1], "chain", behind)

    arriving = jnp.zeros((samples, level_rows), jnp.float32)
    arriving = lax.fori_loop(0, chain - 1, backward_hop, arriving)
    pending_rows, _ = backward_levels(arriving)

    forward_own = []
    answers = []
    for level in range(levels):
        forward_own.append(lax.dynamic_slice_in_dim(solved[level], my_group * sup_rows, sup_rows, 1))
        own_rows = lax.dynamic_slice_in_dim(pending_rows[level], my_group * sup_rows, sup_rows, 1)
        answers.append(matmul(own_rows, inverse_diag[level, 0]))
    forward_own = jnp.stack(forward_own)
    answers = jnp.stack(answers)
    return (forward_own[:, None], answers[:, None])


def solution(mesh):
    return jax.shard_map(
        shards,
        mesh=mesh,
        in_specs=(
            P("chain", "grp", None, None),
            P("chain", "grp", None, None, None),
            P("chain", "grp", None, None),
            P("chain", None, None),
        ),
        out_specs=(P("chain", "grp", None, None), P("chain", "grp", None, None)),
        check_vma=False,
    )
```

```python
import jax
import jax.numpy as jnp
from jax import lax
from jax.sharding import PartitionSpec as P

PRECISE = lax.Precision.HIGHEST


def matmul(left_side, right_factor):
    return jnp.dot(left_side, right_factor, precision=PRECISE, preferred_element_type=jnp.float32)


def matmul_trans(left_side, right_factor):
    return lax.dot_general(
        left_side,
        right_factor,
        (((1,), (1,)), ((), ())),
        precision=PRECISE,
        preferred_element_type=jnp.float32,
    )


TERMS = 3


def split_parts(value, count):
    parts = []
    rest = value
    for _ in range(count):
        part = rest.astype(jnp.bfloat16)
        parts.append(part)
        rest = rest - part.astype(jnp.float32)
    return parts


def term_pairs(count):
    return [(left, right) for left in range(count) for right in range(count) if left + right < count]


def stack_right(value, count):
    parts = split_parts(value, count)
    return jnp.concatenate([parts[right] for _, right in term_pairs(count)], axis=0)


def split_matmul(left_side, stacked):
    count = 2 if TERMS == 3 else 3
    parts = split_parts(left_side, count)
    stacked_left = jnp.concatenate([parts[left] for left, _ in term_pairs(count)], axis=1)
    return jnp.dot(stacked_left, stacked, preferred_element_type=jnp.float32)


def shards(right_side, factor, inverse_diag, pattern):
    levels = right_side.shape[0]
    samples = right_side.shape[2]
    sup_rows = right_side.shape[3]
    groups = lax.axis_size("grp")
    chain = lax.axis_size("chain")
    level_rows = groups * sup_rows
    my_group = lax.axis_index("grp")
    scaled = jnp.einsum(
        "lgti,lgkij->lgktj",
        inverse_diag,
        factor,
        precision=PRECISE,
        preferred_element_type=jnp.float32,
    )
    lifted = jnp.einsum(
        "lgsi,lgti->lgst",
        right_side,
        inverse_diag,
        precision=PRECISE,
        preferred_element_type=jnp.float32,
    )
    blocks, offsets = (
        lax.all_gather(scaled, "grp", axis=1, tiled=True),
        lax.all_gather(lifted, "grp", axis=1, tiled=True),
    )
    onehot = (pattern[..., None] == jnp.arange(groups, dtype=jnp.int32)).astype(jnp.float32)
    level_maps = -jnp.einsum(
        "lgkh,lgktj->lhjgt", onehot, blocks, precision=PRECISE, preferred_element_type=jnp.float32
    )
    level_maps = level_maps.reshape(levels, level_rows, level_rows)
    sources = offsets.transpose(0, 2, 1, 3).reshape(levels, samples, level_rows)

    count = 2 if TERMS == 3 else 3
    forward_stacks = [stack_right(level_maps[level], count) for level in range(levels)]
    backward_stacks = [stack_right(-level_maps[level].T, count) for level in range(levels)]

    def forward_levels(state):
        rows = []
        for level in range(levels):
            state = split_matmul(state, forward_stacks[level]) + sources[level]
            rows.append(state)
        return rows

    ahead = [(position, position + 1) for position in range(chain - 1)]
    behind = [(position + 1, position) for position in range(chain - 1)]

    def forward_hop(_, state):
        return lax.ppermute(forward_levels(state)[-1], "chain", ahead)

    incoming = jnp.zeros((samples, level_rows), jnp.float32)
    incoming = lax.fori_loop(0, chain - 1, forward_hop, incoming, unroll=chain <= 8)
    solved = forward_levels(incoming)

    def backward_levels(running):
        rows = [None] * levels
        for level in reversed(range(levels)):
            rows[level] = solved[level] - running
            running = split_matmul(rows[level], backward_stacks[level])
        return rows, running

    def backward_hop(_, running):
        return lax.ppermute(backward_levels(running)[1], "chain", behind)

    arriving = jnp.zeros((samples, level_rows), jnp.float32)
    arriving = lax.fori_loop(0, chain - 1, backward_hop, arriving, unroll=chain <= 8)
    pending_rows, _ = backward_levels(arriving)

    forward_own = []
    answers = []
    for level in range(levels):
        forward_own.append(lax.dynamic_slice_in_dim(solved[level], my_group * sup_rows, sup_rows, 1))
        own_rows = lax.dynamic_slice_in_dim(pending_rows[level], my_group * sup_rows, sup_rows, 1)
        answers.append(matmul(own_rows, inverse_diag[level, 0]))
    forward_own = jnp.stack(forward_own)
    answers = jnp.stack(answers)
    return (forward_own[:, None], answers[:, None])


def solution(mesh):
    return jax.shard_map(
        shards,
        mesh=mesh,
        in_specs=(
            P("chain", "grp", None, None),
            P("chain", "grp", None, None, None),
            P("chain", "grp", None, None),
            P("chain", None, None),
        ),
        out_specs=(P("chain", "grp", None, None), P("chain", "grp", None, None)),
        check_vma=False,
    )
```

```python
import jax
import jax.numpy as jnp
from jax import lax
from jax.sharding import PartitionSpec as P

PRECISE = lax.Precision.HIGHEST


def matmul(left_side, right_factor):
    return jnp.dot(left_side, right_factor, precision=PRECISE, preferred_element_type=jnp.float32)


def matmul_trans(left_side, right_factor):
    return lax.dot_general(
        left_side,
        right_factor,
        (((1,), (1,)), ((), ())),
        precision=PRECISE,
        preferred_element_type=jnp.float32,
    )


TERMS = 3


def split_parts(value, count):
    parts = []
    rest = value
    for _ in range(count):
        part = rest.astype(jnp.bfloat16)
        parts.append(part)
        rest = rest - part.astype(jnp.float32)
    return parts


def term_pairs(count):
    return [(left, right) for left in range(count) for right in range(count) if left + right < count]


def stack_right(value, count):
    parts = split_parts(value, count)
    return jnp.concatenate([parts[right] for _, right in term_pairs(count)], axis=0)


def split_matmul(left_side, stacked):
    count = 2 if TERMS == 3 else 3
    parts = split_parts(left_side, count)
    stacked_left = jnp.concatenate([parts[left] for left, _ in term_pairs(count)], axis=1)
    return jnp.dot(stacked_left, stacked, preferred_element_type=jnp.float32)


def shards(right_side, factor, inverse_diag, pattern):
    levels = right_side.shape[0]
    samples = right_side.shape[2]
    sup_rows = right_side.shape[3]
    groups = lax.axis_size("grp")
    chain = lax.axis_size("chain")
    level_rows = groups * sup_rows
    my_group = lax.axis_index("grp")
    scaled = jnp.einsum(
        "lgti,lgkij->lgktj",
        inverse_diag,
        factor,
        precision=PRECISE,
        preferred_element_type=jnp.float32,
    )
    lifted = jnp.einsum(
        "lgsi,lgti->lgst",
        right_side,
        inverse_diag,
        precision=PRECISE,
        preferred_element_type=jnp.float32,
    )
    knb = factor.shape[2]
    block_size = knb * sup_rows * sup_rows
    packed = jnp.concatenate([scaled.reshape(levels, -1), lifted.reshape(levels, -1)], axis=1)
    pieces = [packed]
    for shift in range(1, groups):
        pieces.append(lax.ppermute(packed, "grp", [(h, (h + shift) % groups) for h in range(groups)]))
    stacked = jnp.stack(pieces, axis=1)
    blocks = stacked[..., :block_size].reshape(levels, groups, knb, sup_rows, sup_rows)
    offsets = stacked[..., block_size:].reshape(levels, groups, samples, sup_rows)
    slot_group = (my_group - jnp.arange(groups, dtype=jnp.int32)) % groups
    pattern_slots = jnp.take(pattern, slot_group, axis=1)
    onehot = (pattern_slots[..., None] == slot_group).astype(jnp.float32)
    level_maps = -jnp.einsum(
        "lgkh,lgktj->lhjgt", onehot, blocks, precision=PRECISE, preferred_element_type=jnp.float32
    )
    level_maps = level_maps.reshape(levels, level_rows, level_rows)
    sources = offsets.transpose(0, 2, 1, 3).reshape(levels, samples, level_rows)

    count = 2 if TERMS == 3 else 3
    forward_stacks = [stack_right(level_maps[level], count) for level in range(levels)]
    backward_stacks = [stack_right(-level_maps[level].T, count) for level in range(levels)]

    def forward_levels(state):
        rows = []
        for level in range(levels):
            state = split_matmul(state, forward_stacks[level]) + sources[level]
            rows.append(state)
        return rows

    ahead = [(position, position + 1) for position in range(chain - 1)]
    behind = [(position + 1, position) for position in range(chain - 1)]

    def forward_hop(_, state):
        return lax.ppermute(forward_levels(state)[-1], "chain", ahead)

    incoming = jnp.zeros((samples, level_rows), jnp.float32)
    incoming = lax.fori_loop(0, chain - 1, forward_hop, incoming, unroll=chain <= 8)
    solved = forward_levels(incoming)

    def backward_levels(running):
        rows = [None] * levels
        for level in reversed(range(levels)):
            rows[level] = solved[level] - running
            running = split_matmul(rows[level], backward_stacks[level])
        return rows, running

    def backward_hop(_, running):
        return lax.ppermute(backward_levels(running)[1], "chain", behind)

    arriving = jnp.zeros((samples, level_rows), jnp.float32)
    arriving = lax.fori_loop(0, chain - 1, backward_hop, arriving, unroll=chain <= 8)
    pending_rows, _ = backward_levels(arriving)

    forward_own = []
    answers = []
    for level in range(levels):
        forward_own.append(solved[level][:, :sup_rows])
        own_rows = pending_rows[level][:, :sup_rows]
        answers.append(matmul(own_rows, inverse_diag[level, 0]))
    forward_own = jnp.stack(forward_own)
    answers = jnp.stack(answers)
    return (forward_own[:, None], answers[:, None])


def solution(mesh):
    return jax.shard_map(
        shards,
        mesh=mesh,
        in_specs=(
            P("chain", "grp", None, None),
            P("chain", "grp", None, None, None),
            P("chain", "grp", None, None),
            P("chain", None, None),
        ),
        out_specs=(P("chain", "grp", None, None), P("chain", "grp", None, None)),
        check_vma=False,
    )
```

```python
import jax
import jax.numpy as jnp
from jax import lax
from jax.sharding import PartitionSpec as P

PRECISE = lax.Precision.HIGHEST


def matmul(left_side, right_factor):
    return jnp.dot(left_side, right_factor, precision=PRECISE, preferred_element_type=jnp.float32)


def matmul_trans(left_side, right_factor):
    return lax.dot_general(
        left_side,
        right_factor,
        (((1,), (1,)), ((), ())),
        precision=PRECISE,
        preferred_element_type=jnp.float32,
    )


TERMS = 3


def split_parts(value, count):
    parts = []
    rest = value
    for _ in range(count):
        part = rest.astype(jnp.bfloat16)
        parts.append(part)
        rest = rest - part.astype(jnp.float32)
    return parts


def term_pairs(count):
    return [(left, right) for left in range(count) for right in range(count) if left + right < count]


def stack_right(value, count):
    parts = split_parts(value, count)
    return jnp.concatenate([parts[right] for _, right in term_pairs(count)], axis=0)


def split_matmul(left_side, stacked):
    count = 2 if TERMS == 3 else 3
    parts = split_parts(left_side, count)
    stacked_left = jnp.concatenate([parts[left] for left, _ in term_pairs(count)], axis=1)
    return jnp.dot(stacked_left, stacked, preferred_element_type=jnp.float32)


def shards(right_side, factor, inverse_diag, pattern):
    levels = right_side.shape[0]
    samples = right_side.shape[2]
    sup_rows = right_side.shape[3]
    groups = lax.axis_size("grp")
    chain = lax.axis_size("chain")
    level_rows = groups * sup_rows
    my_group = lax.axis_index("grp")
    scaled = jnp.einsum(
        "lgti,lgkij->lgktj",
        inverse_diag,
        factor,
        precision=PRECISE,
        preferred_element_type=jnp.float32,
    )
    lifted = jnp.einsum(
        "lgsi,lgti->lgst",
        right_side,
        inverse_diag,
        precision=PRECISE,
        preferred_element_type=jnp.float32,
    )
    knb = factor.shape[2]
    block_size = knb * sup_rows * sup_rows
    packed = jnp.concatenate([scaled.reshape(levels, -1), lifted.reshape(levels, -1)], axis=1)
    pieces = [packed]
    for shift in range(1, groups):
        pieces.append(lax.ppermute(packed, "grp", [(h, (h + shift) % groups) for h in range(groups)]))
    stacked = jnp.stack(pieces, axis=1)
    blocks = stacked[..., :block_size].reshape(levels, groups, knb, sup_rows, sup_rows)
    offsets = stacked[..., block_size:].reshape(levels, groups, samples, sup_rows)
    slot_group = (my_group - jnp.arange(groups, dtype=jnp.int32)) % groups
    pattern_slots = jnp.take(pattern, slot_group, axis=1)
    onehot = (pattern_slots[..., None] == slot_group).astype(jnp.float32)
    level_maps = -jnp.einsum(
        "lgkh,lgktj->lhjgt", onehot, blocks, precision=PRECISE, preferred_element_type=jnp.float32
    )
    level_maps = level_maps.reshape(levels, level_rows, level_rows)
    sources = offsets.transpose(0, 2, 1, 3).reshape(levels, samples, level_rows)

    count = 2 if TERMS == 3 else 3
    forward_stacks = [stack_right(level_maps[level], count) for level in range(levels)]
    backward_stacks = [stack_right(-level_maps[level].T, count) for level in range(levels)]

    def forward_levels(state):
        rows = []
        for level in range(levels):
            state = split_matmul(state, forward_stacks[level]) + sources[level]
            rows.append(state)
        return rows

    my_chain = lax.axis_index("chain")
    ahead = [(position, position + 1) for position in range(chain - 1)]
    behind = [(position + 1, position) for position in range(chain - 1)]
    ahead_two = [(position, position + 2) for position in range(chain - 2)]
    behind_two = [(position + 2, position) for position in range(chain - 2)]
    skips = max(chain - 2, 0) // 2 + max(chain - 2, 0) % 2
    zeros = jnp.zeros((samples, level_rows), jnp.float32)

    composed = level_maps[0]
    for level in range(1, levels):
        composed = split_matmul(composed, forward_stacks[level])
    packet = jnp.concatenate([composed, forward_levels(zeros)[-1]], axis=0)
    next_packet = lax.ppermute(packet, "chain", behind)
    next_stack = stack_right(next_packet[:level_rows], count)
    next_shift = next_packet[level_rows:]
    previous_map = lax.ppermute(composed, "chain", ahead)
    previous_stack = stack_right(previous_map.T, count)

    def forward_skip(step, state):
        single = forward_levels(state)[-1]
        double = split_matmul(single, next_stack) + next_shift
        from_one = lax.ppermute(single, "chain", ahead)
        from_two = lax.ppermute(double, "chain", ahead_two)
        return jnp.where(my_chain - 1 <= 1 + 2 * step, from_one, from_two)

    incoming = zeros
    if chain > 1:
        incoming = lax.ppermute(forward_levels(incoming)[-1], "chain", ahead)
    incoming = lax.fori_loop(0, skips, forward_skip, incoming, unroll=chain <= 8)
    solved = forward_levels(incoming)

    def backward_levels(running):
        rows = [None] * levels
        for level in reversed(range(levels)):
            rows[level] = solved[level] - running
            running = split_matmul(rows[level], backward_stacks[level])
        return rows, running

    previous_shift = lax.ppermute(backward_levels(zeros)[1], "chain", ahead)
    mirror = chain - 1 - my_chain

    def backward_skip(step, running):
        single = backward_levels(running)[1]
        double = split_matmul(single, previous_stack) + previous_shift
        from_one = lax.ppermute(single, "chain", behind)
        from_two = lax.ppermute(double, "chain", behind_two)
        return jnp.where(mirror - 1 <= 1 + 2 * step, from_one, from_two)

    arriving = zeros
    if chain > 1:
        arriving = lax.ppermute(backward_levels(arriving)[1], "chain", behind)
    arriving = lax.fori_loop(0, skips, backward_skip, arriving, unroll=chain <= 8)
    pending_rows, _ = backward_levels(arriving)

    forward_own = []
    answers = []
    for level in range(levels):
        forward_own.append(solved[level][:, :sup_rows])
        own_rows = pending_rows[level][:, :sup_rows]
        answers.append(matmul(own_rows, inverse_diag[level, 0]))
    forward_own = jnp.stack(forward_own)
    answers = jnp.stack(answers)
    return (forward_own[:, None], answers[:, None])


def solution(mesh):
    return jax.shard_map(
        shards,
        mesh=mesh,
        in_specs=(
            P("chain", "grp", None, None),
            P("chain", "grp", None, None, None),
            P("chain", "grp", None, None),
            P("chain", None, None),
        ),
        out_specs=(P("chain", "grp", None, None), P("chain", "grp", None, None)),
        check_vma=False,
    )
```

```python
import jax
import jax.numpy as jnp
from jax import lax
from jax.sharding import PartitionSpec as P

PRECISE = lax.Precision.HIGHEST


def matmul(left_side, right_factor):
    return jnp.dot(left_side, right_factor, precision=PRECISE, preferred_element_type=jnp.float32)


def matmul_trans(left_side, right_factor):
    return lax.dot_general(
        left_side,
        right_factor,
        (((1,), (1,)), ((), ())),
        precision=PRECISE,
        preferred_element_type=jnp.float32,
    )


TERMS = 3


def split_parts(value, count):
    parts = []
    rest = value
    for _ in range(count):
        part = rest.astype(jnp.bfloat16)
        parts.append(part)
        rest = rest - part.astype(jnp.float32)
    return parts


def term_pairs(count):
    return [(left, right) for left in range(count) for right in range(count) if left + right < count]


def stack_right(value, count):
    parts = split_parts(value, count)
    return jnp.concatenate([parts[right] for _, right in term_pairs(count)], axis=0)


def split_matmul(left_side, stacked):
    count = 2 if TERMS == 3 else 3
    parts = split_parts(left_side, count)
    stacked_left = jnp.concatenate([parts[left] for left, _ in term_pairs(count)], axis=1)
    return jnp.dot(stacked_left, stacked, preferred_element_type=jnp.float32)


def shards(right_side, factor, inverse_diag, pattern):
    levels = right_side.shape[0]
    samples = right_side.shape[2]
    sup_rows = right_side.shape[3]
    groups = lax.axis_size("grp")
    chain = lax.axis_size("chain")
    level_rows = groups * sup_rows
    my_group = lax.axis_index("grp")
    scaled = jnp.einsum(
        "lgti,lgkij->lgktj",
        inverse_diag,
        factor,
        precision=PRECISE,
        preferred_element_type=jnp.float32,
    )
    lifted = jnp.einsum(
        "lgsi,lgti->lgst",
        right_side,
        inverse_diag,
        precision=PRECISE,
        preferred_element_type=jnp.float32,
    )
    knb = factor.shape[2]
    block_size = knb * sup_rows * sup_rows
    my_chain = lax.axis_index("chain")
    is_odd = my_chain % 2 == 1
    packed = jnp.concatenate([scaled.reshape(levels, -1), lifted.reshape(levels, -1)], axis=1)
    own_pieces = [packed]
    for shift in range(1, groups):
        own_pieces.append(lax.ppermute(packed, "grp", [(h, (h + shift) % groups) for h in range(groups)]))
    partner_pieces = []
    for shift in range(groups):
        pairs = [
            (position * groups + h, (position ^ 1) * groups + (h + shift) % groups)
            for position in range(chain)
            for h in range(groups)
        ]
        partner_pieces.append(lax.ppermute(packed, ("chain", "grp"), pairs))
    swap = [(position, position ^ 1) for position in range(chain)]
    partner_pattern = lax.ppermute(pattern, "chain", swap)
    own_stacked = jnp.stack(own_pieces, axis=1)
    partner_stacked = jnp.stack(partner_pieces, axis=1)
    pair_stacked = jnp.concatenate(
        [jnp.where(is_odd, partner_stacked, own_stacked), jnp.where(is_odd, own_stacked, partner_stacked)], axis=0
    )
    pair_pattern = jnp.concatenate(
        [jnp.where(is_odd, partner_pattern, pattern), jnp.where(is_odd, pattern, partner_pattern)], axis=0
    )
    pair_levels = 2 * levels
    blocks = pair_stacked[..., :block_size].reshape(pair_levels, groups, knb, sup_rows, sup_rows)
    offsets = pair_stacked[..., block_size:].reshape(pair_levels, groups, samples, sup_rows)
    slot_group = (my_group - jnp.arange(groups, dtype=jnp.int32)) % groups
    pattern_slots = jnp.take(pair_pattern, slot_group, axis=1)
    onehot = (pattern_slots[..., None] == slot_group).astype(jnp.float32)
    level_maps = -jnp.einsum(
        "lgkh,lgktj->lhjgt", onehot, blocks, precision=PRECISE, preferred_element_type=jnp.float32
    )
    level_maps = level_maps.reshape(pair_levels, level_rows, level_rows)
    sources = offsets.transpose(0, 2, 1, 3).reshape(pair_levels, samples, level_rows)

    count = 2 if TERMS == 3 else 3
    forward_stacks = [stack_right(level_maps[level], count) for level in range(pair_levels)]
    backward_stacks = [stack_right(-level_maps[level].T, count) for level in range(pair_levels)]

    def forward_levels(state):
        rows = []
        for level in range(pair_levels):
            state = split_matmul(state, forward_stacks[level]) + sources[level]
            rows.append(state)
        return rows

    pair_count = chain // 2
    evens = [(2 * pair, 2 * pair + 2) for pair in range(pair_count - 1)]
    odds = [(2 * pair + 3, 2 * pair + 1) for pair in range(pair_count - 1)]
    to_odd = [(2 * pair, 2 * pair + 1) for pair in range(pair_count)]
    to_even = [(2 * pair + 1, 2 * pair) for pair in range(pair_count)]

    def forward_hop(_, state):
        return lax.ppermute(forward_levels(state)[-1], "chain", evens)

    incoming = jnp.zeros((samples, level_rows), jnp.float32)
    incoming = lax.fori_loop(0, pair_count - 1, forward_hop, incoming, unroll=chain <= 8)
    incoming = jnp.where(is_odd, lax.ppermute(incoming, "chain", to_odd), incoming)
    solved = forward_levels(incoming)

    def backward_levels(running):
        rows = [None] * pair_levels
        for level in reversed(range(pair_levels)):
            rows[level] = solved[level] - running
            running = split_matmul(rows[level], backward_stacks[level])
        return rows, running

    def backward_hop(_, running):
        return lax.ppermute(backward_levels(running)[1], "chain", odds)

    arriving = jnp.zeros((samples, level_rows), jnp.float32)
    arriving = lax.fori_loop(0, pair_count - 1, backward_hop, arriving, unroll=chain <= 8)
    arriving = jnp.where(is_odd, arriving, lax.ppermute(arriving, "chain", to_even))
    pending_rows, _ = backward_levels(arriving)

    forward_pair = jnp.stack([rows[:, :sup_rows] for rows in solved])
    pending_pair = jnp.stack([rows[:, :sup_rows] for rows in pending_rows])
    forward_own = jnp.where(is_odd, forward_pair[levels:], forward_pair[:levels])
    pending_own = jnp.where(is_odd, pending_pair[levels:], pending_pair[:levels])
    answers = jnp.stack([matmul(pending_own[level], inverse_diag[level, 0]) for level in range(levels)])
    return (forward_own[:, None], answers[:, None])


def solution(mesh):
    return jax.shard_map(
        shards,
        mesh=mesh,
        in_specs=(
            P("chain", "grp", None, None),
            P("chain", "grp", None, None, None),
            P("chain", "grp", None, None),
            P("chain", None, None),
        ),
        out_specs=(P("chain", "grp", None, None), P("chain", "grp", None, None)),
        check_vma=False,
    )
```

```python
import jax
import jax.numpy as jnp
from jax import lax
from jax.sharding import PartitionSpec as P

PRECISE = lax.Precision.HIGHEST


def matmul(left_side, right_factor):
    return jnp.dot(left_side, right_factor, precision=PRECISE, preferred_element_type=jnp.float32)


def matmul_trans(left_side, right_factor):
    return lax.dot_general(
        left_side,
        right_factor,
        (((1,), (1,)), ((), ())),
        precision=PRECISE,
        preferred_element_type=jnp.float32,
    )


TERMS = 3


def split_parts(value, count):
    parts = []
    rest = value
    for _ in range(count):
        part = rest.astype(jnp.bfloat16)
        parts.append(part)
        rest = rest - part.astype(jnp.float32)
    return parts


def term_pairs(count):
    return [(left, right) for left in range(count) for right in range(count) if left + right < count]


def stack_right(value, count):
    parts = split_parts(value, count)
    return jnp.concatenate([parts[right] for _, right in term_pairs(count)], axis=0)


def split_matmul(left_side, stacked):
    count = 2 if TERMS == 3 else 3
    parts = split_parts(left_side, count)
    stacked_left = jnp.concatenate([parts[left] for left, _ in term_pairs(count)], axis=1)
    return jnp.dot(stacked_left, stacked, preferred_element_type=jnp.float32)


def shards(right_side, factor, inverse_diag, pattern):
    levels = right_side.shape[0]
    samples = right_side.shape[2]
    sup_rows = right_side.shape[3]
    groups = lax.axis_size("grp")
    chain = lax.axis_size("chain")
    level_rows = groups * sup_rows
    my_group = lax.axis_index("grp")
    scaled = jnp.einsum(
        "lgti,lgkij->lgktj",
        inverse_diag,
        factor,
        precision=PRECISE,
        preferred_element_type=jnp.float32,
    )
    lifted = jnp.einsum(
        "lgsi,lgti->lgst",
        right_side,
        inverse_diag,
        precision=PRECISE,
        preferred_element_type=jnp.float32,
    )
    knb = factor.shape[2]
    block_size = knb * sup_rows * sup_rows
    my_chain = lax.axis_index("chain")
    is_odd = my_chain % 2 == 1
    packed = jnp.concatenate([scaled.reshape(levels, -1), lifted.reshape(levels, -1)], axis=1)
    own_pieces = [packed]
    for shift in range(1, groups):
        own_pieces.append(lax.ppermute(packed, "grp", [(h, (h + shift) % groups) for h in range(groups)]))
    partner_pieces = []
    for shift in range(groups):
        pairs = [
            (position * groups + h, (position ^ 1) * groups + (h + shift) % groups)
            for position in range(chain)
            for h in range(groups)
        ]
        partner_pieces.append(lax.ppermute(packed, ("chain", "grp"), pairs))
    swap = [(position, position ^ 1) for position in range(chain)]
    partner_pattern = lax.ppermute(pattern, "chain", swap)
    own_stacked = jnp.stack(own_pieces, axis=1)
    partner_stacked = jnp.stack(partner_pieces, axis=1)
    pair_stacked = jnp.concatenate(
        [jnp.where(is_odd, partner_stacked, own_stacked), jnp.where(is_odd, own_stacked, partner_stacked)], axis=0
    )
    pair_pattern = jnp.concatenate(
        [jnp.where(is_odd, partner_pattern, pattern), jnp.where(is_odd, pattern, partner_pattern)], axis=0
    )
    pair_levels = 2 * levels
    blocks = pair_stacked[..., :block_size].reshape(pair_levels, groups, knb, sup_rows, sup_rows)
    offsets = pair_stacked[..., block_size:].reshape(pair_levels, groups, samples, sup_rows)
    slot_group = (my_group - jnp.arange(groups, dtype=jnp.int32)) % groups
    pattern_slots = jnp.take(pair_pattern, slot_group, axis=1)
    onehot = (pattern_slots[..., None] == slot_group).astype(jnp.float32)
    coupling = jnp.einsum(
        "lgkh,lgktj->lgthj", onehot, blocks, precision=PRECISE, preferred_element_type=jnp.float32
    )
    coupling = coupling.reshape(pair_levels, level_rows, level_rows)
    sources = offsets.transpose(0, 2, 1, 3).reshape(pair_levels, samples, level_rows)

    count = 2 if TERMS == 3 else 3
    forward_stacks = []
    backward_stacks = []
    for level in range(pair_levels):
        parts = split_parts(coupling[level], count)
        chosen = [parts[right] for _, right in term_pairs(count)]
        forward_stacks.append(jnp.concatenate(chosen, axis=1))
        backward_stacks.append(jnp.concatenate(chosen, axis=0))

    def forward_product(state, stacked):
        left_parts = split_parts(state, count)
        stacked_left = jnp.concatenate([left_parts[left] for left, _ in term_pairs(count)], axis=1)
        return lax.dot_general(
            stacked_left, stacked, (((1,), (1,)), ((), ())), preferred_element_type=jnp.float32
        )

    def forward_levels(state):
        rows = []
        for level in range(pair_levels):
            state = sources[level] - forward_product(state, forward_stacks[level])
            rows.append(state)
        return rows

    pair_count = chain // 2
    evens = [(2 * pair, 2 * pair + 2) for pair in range(pair_count - 1)]
    odds = [(2 * pair + 3, 2 * pair + 1) for pair in range(pair_count - 1)]
    to_odd = [(2 * pair, 2 * pair + 1) for pair in range(pair_count)]
    to_even = [(2 * pair + 1, 2 * pair) for pair in range(pair_count)]

    def forward_hop(_, state):
        return lax.ppermute(forward_levels(state)[-1], "chain", evens)

    incoming = jnp.zeros((samples, level_rows), jnp.float32)
    incoming = lax.fori_loop(0, pair_count - 1, forward_hop, incoming, unroll=chain <= 8)
    incoming = jnp.where(is_odd, lax.ppermute(incoming, "chain", to_odd), incoming)
    solved = forward_levels(incoming)

    def backward_levels(running):
        rows = [None] * pair_levels
        for level in reversed(range(pair_levels)):
            rows[level] = solved[level] - running
            running = split_matmul(rows[level], backward_stacks[level])
        return rows, running

    def backward_hop(_, running):
        return lax.ppermute(backward_levels(running)[1], "chain", odds)

    arriving = jnp.zeros((samples, level_rows), jnp.float32)
    arriving = lax.fori_loop(0, pair_count - 1, backward_hop, arriving, unroll=chain <= 8)
    arriving = jnp.where(is_odd, arriving, lax.ppermute(arriving, "chain", to_even))
    pending_rows, _ = backward_levels(arriving)

    forward_pair = jnp.stack([rows[:, :sup_rows] for rows in solved])
    pending_pair = jnp.stack([rows[:, :sup_rows] for rows in pending_rows])
    forward_own = jnp.where(is_odd, forward_pair[levels:], forward_pair[:levels])
    pending_own = jnp.where(is_odd, pending_pair[levels:], pending_pair[:levels])
    answers = jnp.stack([matmul(pending_own[level], inverse_diag[level, 0]) for level in range(levels)])
    return (forward_own[:, None], answers[:, None])


def solution(mesh):
    return jax.shard_map(
        shards,
        mesh=mesh,
        in_specs=(
            P("chain", "grp", None, None),
            P("chain", "grp", None, None, None),
            P("chain", "grp", None, None),
            P("chain", None, None),
        ),
        out_specs=(P("chain", "grp", None, None), P("chain", "grp", None, None)),
        check_vma=False,
    )
```

```python
import jax
import jax.numpy as jnp
from jax import lax
from jax.sharding import PartitionSpec as P

PRECISE = lax.Precision.HIGHEST


def matmul(left_side, right_factor):
    return jnp.dot(left_side, right_factor, precision=PRECISE, preferred_element_type=jnp.float32)


def matmul_trans(left_side, right_factor):
    return lax.dot_general(
        left_side,
        right_factor,
        (((1,), (1,)), ((), ())),
        precision=PRECISE,
        preferred_element_type=jnp.float32,
    )


TERMS = 3


def split_parts(value, count):
    parts = []
    rest = value
    for _ in range(count):
        part = rest.astype(jnp.bfloat16)
        parts.append(part)
        rest = rest - part.astype(jnp.float32)
    return parts


def term_pairs(count):
    return [(left, right) for left in range(count) for right in range(count) if left + right < count]


def stack_right(value, count):
    parts = split_parts(value, count)
    return jnp.concatenate([parts[right] for _, right in term_pairs(count)], axis=0)


def split_matmul(left_side, stacked):
    count = 2 if TERMS == 3 else 3
    parts = split_parts(left_side, count)
    stacked_left = jnp.concatenate([parts[left] for left, _ in term_pairs(count)], axis=1)
    return jnp.dot(stacked_left, stacked, preferred_element_type=jnp.float32)


def shards(right_side, factor, inverse_diag, pattern):
    levels = right_side.shape[0]
    samples = right_side.shape[2]
    sup_rows = right_side.shape[3]
    groups = lax.axis_size("grp")
    chain = lax.axis_size("chain")
    level_rows = groups * sup_rows
    my_group = lax.axis_index("grp")
    scaled = jnp.einsum(
        "lgti,lgkij->lgktj",
        inverse_diag,
        factor,
        precision=PRECISE,
        preferred_element_type=jnp.float32,
    )
    lifted = jnp.einsum(
        "lgsi,lgti->lgst",
        right_side,
        inverse_diag,
        precision=PRECISE,
        preferred_element_type=jnp.float32,
    )
    knb = factor.shape[2]
    block_size = knb * sup_rows * sup_rows
    my_chain = lax.axis_index("chain")
    is_odd = my_chain % 2 == 1
    packed = jnp.concatenate([scaled.reshape(levels, -1), lifted.reshape(levels, -1)], axis=1)
    own_pieces = [packed]
    for shift in range(1, groups):
        own_pieces.append(lax.ppermute(packed, "grp", [(h, (h + shift) % groups) for h in range(groups)]))
    partner_pieces = []
    for shift in range(groups):
        pairs = [
            (position * groups + h, (position ^ 1) * groups + (h + shift) % groups)
            for position in range(chain)
            for h in range(groups)
        ]
        partner_pieces.append(lax.ppermute(packed, ("chain", "grp"), pairs))
    swap = [(position, position ^ 1) for position in range(chain)]
    partner_pattern = lax.ppermute(pattern, "chain", swap)
    own_stacked = jnp.stack(own_pieces, axis=1)
    partner_stacked = jnp.stack(partner_pieces, axis=1)
    pair_stacked = jnp.concatenate(
        [jnp.where(is_odd, partner_stacked, own_stacked), jnp.where(is_odd, own_stacked, partner_stacked)], axis=0
    )
    pair_pattern = jnp.concatenate(
        [jnp.where(is_odd, partner_pattern, pattern), jnp.where(is_odd, pattern, partner_pattern)], axis=0
    )
    pair_levels = 2 * levels
    blocks = pair_stacked[..., :block_size].reshape(pair_levels, groups, knb, sup_rows, sup_rows)
    offsets = pair_stacked[..., block_size:].reshape(pair_levels, groups, samples, sup_rows)
    slot_group = (my_group - jnp.arange(groups, dtype=jnp.int32)) % groups
    pattern_slots = jnp.take(pair_pattern, slot_group, axis=1)
    chosen_slots = pattern_slots[..., None] == slot_group
    sources = offsets.transpose(0, 2, 1, 3).reshape(pair_levels, samples, level_rows)

    count = 2 if TERMS == 3 else 3
    block_parts = split_parts(blocks, count)

    def coupling_part(part):
        placed = jnp.zeros((pair_levels, groups, sup_rows, groups, sup_rows), jnp.bfloat16)
        for k in range(knb):
            placed = placed + jnp.where(
                chosen_slots[:, :, k, None, :, None], part[:, :, k, :, None, :], jnp.zeros((), jnp.bfloat16)
            )
        return placed.reshape(pair_levels, level_rows, level_rows)

    coupling_parts = [coupling_part(part) for part in block_parts]
    chosen = [coupling_parts[right] for _, right in term_pairs(count)]
    forward_all = jnp.concatenate(chosen, axis=2)
    backward_all = jnp.concatenate(chosen, axis=1)
    forward_stacks = [forward_all[level] for level in range(pair_levels)]
    backward_stacks = [backward_all[level] for level in range(pair_levels)]

    def forward_product(state, stacked):
        left_parts = split_parts(state, count)
        stacked_left = jnp.concatenate([left_parts[left] for left, _ in term_pairs(count)], axis=1)
        return lax.dot_general(
            stacked_left, stacked, (((1,), (1,)), ((), ())), preferred_element_type=jnp.float32
        )

    def forward_levels(state):
        rows = []
        for level in range(pair_levels):
            state = sources[level] - forward_product(state, forward_stacks[level])
            rows.append(state)
        return rows

    pair_count = chain // 2
    evens = [(2 * pair, 2 * pair + 2) for pair in range(pair_count - 1)]
    odds = [(2 * pair + 3, 2 * pair + 1) for pair in range(pair_count - 1)]
    to_odd = [(2 * pair, 2 * pair + 1) for pair in range(pair_count)]
    to_even = [(2 * pair + 1, 2 * pair) for pair in range(pair_count)]

    def forward_hop(_, state):
        return lax.ppermute(forward_levels(state)[-1], "chain", evens)

    incoming = jnp.zeros((samples, level_rows), jnp.float32)
    incoming = lax.fori_loop(0, pair_count - 1, forward_hop, incoming, unroll=chain <= 8)
    incoming = jnp.where(is_odd, lax.ppermute(incoming, "chain", to_odd), incoming)
    solved = forward_levels(incoming)

    def backward_levels(running):
        rows = [None] * pair_levels
        for level in reversed(range(pair_levels)):
            rows[level] = solved[level] - running
            running = split_matmul(rows[level], backward_stacks[level])
        return rows, running

    def backward_hop(_, running):
        return lax.ppermute(backward_levels(running)[1], "chain", odds)

    arriving = jnp.zeros((samples, level_rows), jnp.float32)
    arriving = lax.fori_loop(0, pair_count - 1, backward_hop, arriving, unroll=chain <= 8)
    arriving = jnp.where(is_odd, arriving, lax.ppermute(arriving, "chain", to_even))
    pending_rows, _ = backward_levels(arriving)

    forward_pair = jnp.stack([rows[:, :sup_rows] for rows in solved])
    pending_pair = jnp.stack([rows[:, :sup_rows] for rows in pending_rows])
    forward_own = jnp.where(is_odd, forward_pair[levels:], forward_pair[:levels])
    pending_own = jnp.where(is_odd, pending_pair[levels:], pending_pair[:levels])
    answers = jnp.stack([matmul(pending_own[level], inverse_diag[level, 0]) for level in range(levels)])
    return (forward_own[:, None], answers[:, None])


def solution(mesh):
    return jax.shard_map(
        shards,
        mesh=mesh,
        in_specs=(
            P("chain", "grp", None, None),
            P("chain", "grp", None, None, None),
            P("chain", "grp", None, None),
            P("chain", None, None),
        ),
        out_specs=(P("chain", "grp", None, None), P("chain", "grp", None, None)),
        check_vma=False,
    )
```

```python
import jax
import jax.numpy as jnp
from jax import lax
from jax.sharding import PartitionSpec as P

PRECISE = lax.Precision.HIGHEST


def matmul(left_side, right_factor):
    return jnp.dot(left_side, right_factor, precision=PRECISE, preferred_element_type=jnp.float32)


def matmul_trans(left_side, right_factor):
    return lax.dot_general(
        left_side,
        right_factor,
        (((1,), (1,)), ((), ())),
        precision=PRECISE,
        preferred_element_type=jnp.float32,
    )


TERMS = 3


def split_parts(value, count):
    parts = []
    rest = value
    for _ in range(count):
        part = rest.astype(jnp.bfloat16)
        parts.append(part)
        rest = rest - part.astype(jnp.float32)
    return parts


def term_pairs(count):
    return [(left, right) for left in range(count) for right in range(count) if left + right < count]


def stack_right(value, count):
    parts = split_parts(value, count)
    return jnp.concatenate([parts[right] for _, right in term_pairs(count)], axis=0)


def split_matmul(left_side, stacked):
    count = 2 if TERMS == 3 else 3
    parts = split_parts(left_side, count)
    stacked_left = jnp.concatenate([parts[left] for left, _ in term_pairs(count)], axis=1)
    return jnp.dot(stacked_left, stacked, preferred_element_type=jnp.float32)


def shards(right_side, factor, inverse_diag, pattern):
    levels = right_side.shape[0]
    samples = right_side.shape[2]
    sup_rows = right_side.shape[3]
    groups = lax.axis_size("grp")
    chain = lax.axis_size("chain")
    level_rows = groups * sup_rows
    my_group = lax.axis_index("grp")
    scaled = jnp.einsum(
        "lgti,lgkij->lgktj",
        inverse_diag,
        factor,
        precision=PRECISE,
        preferred_element_type=jnp.float32,
    )
    lifted = jnp.einsum(
        "lgsi,lgti->lgst",
        right_side,
        inverse_diag,
        precision=PRECISE,
        preferred_element_type=jnp.float32,
    )
    knb = factor.shape[2]
    block_size = knb * sup_rows * sup_rows
    my_chain = lax.axis_index("chain")
    is_odd = my_chain % 2 == 1
    packed = jnp.concatenate([scaled.reshape(levels, -1), lifted.reshape(levels, -1)], axis=1)
    own_pieces = [packed]
    for shift in range(1, groups):
        own_pieces.append(lax.ppermute(packed, "grp", [(h, (h + shift) % groups) for h in range(groups)]))
    partner_pieces = []
    for shift in range(groups):
        pairs = [
            (position * groups + h, (position ^ 1) * groups + (h + shift) % groups)
            for position in range(chain)
            for h in range(groups)
        ]
        partner_pieces.append(lax.ppermute(packed, ("chain", "grp"), pairs))
    swap = [(position, position ^ 1) for position in range(chain)]
    partner_pattern = lax.ppermute(pattern, "chain", swap)
    own_stacked = jnp.stack(own_pieces, axis=1)
    partner_stacked = jnp.stack(partner_pieces, axis=1)
    pair_stacked = jnp.concatenate(
        [jnp.where(is_odd, partner_stacked, own_stacked), jnp.where(is_odd, own_stacked, partner_stacked)], axis=0
    )
    pair_pattern = jnp.concatenate(
        [jnp.where(is_odd, partner_pattern, pattern), jnp.where(is_odd, pattern, partner_pattern)], axis=0
    )
    pair_levels = 2 * levels
    blocks = pair_stacked[..., :block_size].reshape(pair_levels, groups, knb, sup_rows, sup_rows)
    offsets = pair_stacked[..., block_size:].reshape(pair_levels, groups, samples, sup_rows)
    slot_group = (my_group - jnp.arange(groups, dtype=jnp.int32)) % groups
    pattern_slots = jnp.take(pair_pattern, slot_group, axis=1)
    onehot = (pattern_slots[..., None] == slot_group).astype(jnp.float32)
    coupling = jnp.einsum(
        "lgkh,lgktj->lgthj", onehot, blocks, precision=PRECISE, preferred_element_type=jnp.float32
    )
    coupling = coupling.reshape(pair_levels, level_rows, level_rows)
    sources = offsets.transpose(0, 2, 1, 3).reshape(pair_levels, samples, level_rows)

    count = 2 if TERMS == 3 else 3
    chosen_parts = []
    forward_stacks = []
    for level in range(pair_levels):
        parts = split_parts(coupling[level], count)
        chosen_parts.append([parts[right] for _, right in term_pairs(count)])
        forward_stacks.append(jnp.concatenate(chosen_parts[-1], axis=1))

    def forward_product(state, stacked):
        left_parts = split_parts(state, count)
        stacked_left = jnp.concatenate([left_parts[left] for left, _ in term_pairs(count)], axis=1)
        return lax.dot_general(
            stacked_left, stacked, (((1,), (1,)), ((), ())), preferred_element_type=jnp.float32
        )

    def forward_levels(state):
        rows = []
        for level in range(pair_levels):
            state = sources[level] - forward_product(state, forward_stacks[level])
            rows.append(state)
        return rows

    pair_count = chain // 2
    evens = [(2 * pair, 2 * pair + 2) for pair in range(pair_count - 1)]
    odds = [(2 * pair + 3, 2 * pair + 1) for pair in range(pair_count - 1)]
    to_odd = [(2 * pair, 2 * pair + 1) for pair in range(pair_count)]
    to_even = [(2 * pair + 1, 2 * pair) for pair in range(pair_count)]

    def forward_hop(_, state):
        return lax.ppermute(forward_levels(state)[-1], "chain", evens)

    incoming = jnp.zeros((samples, level_rows), jnp.float32)
    if pair_count > 1:
        first_out = forward_levels(incoming)[-1]
        incoming = lax.ppermute(first_out, "chain", evens)
        chosen_parts, _ = lax.optimization_barrier((chosen_parts, first_out))
    backward_stacks = [jnp.concatenate(chosen, axis=0) for chosen in chosen_parts]
    incoming = lax.fori_loop(1, pair_count - 1, forward_hop, incoming, unroll=chain <= 8)
    incoming = jnp.where(is_odd, lax.ppermute(incoming, "chain", to_odd), incoming)
    solved = forward_levels(incoming)

    def backward_levels(running):
        rows = [None] * pair_levels
        for level in reversed(range(pair_levels)):
            rows[level] = solved[level] - running
            running = split_matmul(rows[level], backward_stacks[level])
        return rows, running

    def backward_hop(_, running):
        return lax.ppermute(backward_levels(running)[1], "chain", odds)

    arriving = jnp.zeros((samples, level_rows), jnp.float32)
    arriving = lax.fori_loop(0, pair_count - 1, backward_hop, arriving, unroll=chain <= 8)
    arriving = jnp.where(is_odd, arriving, lax.ppermute(arriving, "chain", to_even))
    pending_rows, _ = backward_levels(arriving)

    forward_pair = jnp.stack([rows[:, :sup_rows] for rows in solved])
    pending_pair = jnp.stack([rows[:, :sup_rows] for rows in pending_rows])
    forward_own = jnp.where(is_odd, forward_pair[levels:], forward_pair[:levels])
    pending_own = jnp.where(is_odd, pending_pair[levels:], pending_pair[:levels])
    answers = jnp.stack([matmul(pending_own[level], inverse_diag[level, 0]) for level in range(levels)])
    return (forward_own[:, None], answers[:, None])


def solution(mesh):
    return jax.shard_map(
        shards,
        mesh=mesh,
        in_specs=(
            P("chain", "grp", None, None),
            P("chain", "grp", None, None, None),
            P("chain", "grp", None, None),
            P("chain", None, None),
        ),
        out_specs=(P("chain", "grp", None, None), P("chain", "grp", None, None)),
        check_vma=False,
    )
```

```python
import jax
import jax.numpy as jnp
from jax import lax
from jax.sharding import PartitionSpec as P

PRECISE = lax.Precision.HIGHEST


def matmul(left_side, right_factor):
    return jnp.dot(left_side, right_factor, precision=PRECISE, preferred_element_type=jnp.float32)


def matmul_trans(left_side, right_factor):
    return lax.dot_general(
        left_side,
        right_factor,
        (((1,), (1,)), ((), ())),
        precision=PRECISE,
        preferred_element_type=jnp.float32,
    )


TERMS = 3


def split_parts(value, count):
    parts = []
    rest = value
    for _ in range(count):
        part = rest.astype(jnp.bfloat16)
        parts.append(part)
        rest = rest - part.astype(jnp.float32)
    return parts


def term_pairs(count):
    return [(left, right) for left in range(count) for right in range(count) if left + right < count]


def stack_right(value, count):
    parts = split_parts(value, count)
    return jnp.concatenate([parts[right] for _, right in term_pairs(count)], axis=0)


def split_matmul(left_side, stacked):
    count = 2 if TERMS == 3 else 3
    parts = split_parts(left_side, count)
    stacked_left = jnp.concatenate([parts[left] for left, _ in term_pairs(count)], axis=1)
    return jnp.dot(stacked_left, stacked, preferred_element_type=jnp.float32)


def shards(right_side, factor, inverse_diag, pattern):
    levels = right_side.shape[0]
    samples = right_side.shape[2]
    sup_rows = right_side.shape[3]
    groups = lax.axis_size("grp")
    chain = lax.axis_size("chain")
    level_rows = groups * sup_rows
    my_group = lax.axis_index("grp")
    scaled = jnp.einsum(
        "lgti,lgkij->lgktj",
        inverse_diag,
        factor,
        precision=PRECISE,
        preferred_element_type=jnp.float32,
    )
    lifted = jnp.einsum(
        "lgsi,lgti->lgst",
        right_side,
        inverse_diag,
        precision=PRECISE,
        preferred_element_type=jnp.float32,
    )
    knb = factor.shape[2]
    block_size = knb * sup_rows * sup_rows
    my_chain = lax.axis_index("chain")
    is_odd = my_chain % 2 == 1
    packed = jnp.concatenate([scaled.reshape(levels, -1), lifted.reshape(levels, -1)], axis=1)
    own_pieces = [packed]
    for shift in range(1, groups):
        own_pieces.append(lax.ppermute(packed, "grp", [(h, (h + shift) % groups) for h in range(groups)]))
    partner_pieces = []
    for shift in range(groups):
        pairs = [
            (position * groups + h, (position ^ 1) * groups + (h + shift) % groups)
            for position in range(chain)
            for h in range(groups)
        ]
        partner_pieces.append(lax.ppermute(packed, ("chain", "grp"), pairs))
    swap = [(position, position ^ 1) for position in range(chain)]
    partner_pattern = lax.ppermute(pattern, "chain", swap)
    own_stacked = jnp.stack(own_pieces, axis=1)
    partner_stacked = jnp.stack(partner_pieces, axis=1)
    pair_stacked = jnp.concatenate(
        [jnp.where(is_odd, partner_stacked, own_stacked), jnp.where(is_odd, own_stacked, partner_stacked)], axis=0
    )
    pair_pattern = jnp.concatenate(
        [jnp.where(is_odd, partner_pattern, pattern), jnp.where(is_odd, pattern, partner_pattern)], axis=0
    )
    pair_levels = 2 * levels
    blocks = pair_stacked[..., :block_size].reshape(pair_levels, groups, knb, sup_rows, sup_rows)
    offsets = pair_stacked[..., block_size:].reshape(pair_levels, groups, samples, sup_rows)
    slot_group = (my_group - jnp.arange(groups, dtype=jnp.int32)) % groups
    pattern_slots = jnp.take(pair_pattern, slot_group, axis=1)
    onehot = (pattern_slots[..., None] == slot_group).astype(jnp.float32)
    coupling = jnp.einsum(
        "lgkh,lgktj->lgthj", onehot, blocks, precision=PRECISE, preferred_element_type=jnp.float32
    )
    coupling = coupling.reshape(pair_levels, level_rows, level_rows)
    sources = offsets.transpose(0, 2, 1, 3).reshape(pair_levels, samples, level_rows)

    count = 2 if TERMS == 3 else 3
    chosen_parts = []
    forward_stacks = []
    for level in range(pair_levels):
        chosen_parts.append(split_parts(coupling[level], 2))
        forward_stacks.append(jnp.concatenate(chosen_parts[-1], axis=1))

    def row_stacked(state):
        high, low = split_parts(state, 2)
        return jnp.concatenate(
            [jnp.concatenate([high, high], axis=1), jnp.concatenate([low, jnp.zeros_like(low)], axis=1)], axis=0
        )

    def paired_matmul(state, stacked):
        out = jnp.dot(row_stacked(state), stacked, preferred_element_type=jnp.float32)
        return out[:samples] + out[samples:]

    def forward_product(state, stacked):
        out = lax.dot_general(
            row_stacked(state), stacked, (((1,), (1,)), ((), ())), preferred_element_type=jnp.float32
        )
        return out[:samples] + out[samples:]

    def forward_levels(state):
        rows = []
        for level in range(pair_levels):
            state = sources[level] - forward_product(state, forward_stacks[level])
            rows.append(state)
        return rows

    pair_count = chain // 2
    evens = [(2 * pair, 2 * pair + 2) for pair in range(pair_count - 1)]
    odds = [(2 * pair + 3, 2 * pair + 1) for pair in range(pair_count - 1)]
    to_odd = [(2 * pair, 2 * pair + 1) for pair in range(pair_count)]
    to_even = [(2 * pair + 1, 2 * pair) for pair in range(pair_count)]

    def forward_hop(_, state):
        return lax.ppermute(forward_levels(state)[-1], "chain", evens)

    incoming = jnp.zeros((samples, level_rows), jnp.float32)
    if pair_count > 1:
        first_out = forward_levels(incoming)[-1]
        incoming = lax.ppermute(first_out, "chain", evens)
        chosen_parts, _ = lax.optimization_barrier((chosen_parts, first_out))
    backward_stacks = [jnp.concatenate(chosen, axis=0) for chosen in chosen_parts]
    incoming = lax.fori_loop(1, pair_count - 1, forward_hop, incoming, unroll=chain <= 8)
    incoming = jnp.where(is_odd, lax.ppermute(incoming, "chain", to_odd), incoming)
    solved = forward_levels(incoming)

    def backward_levels(running):
        rows = [None] * pair_levels
        for level in reversed(range(pair_levels)):
            rows[level] = solved[level] - running
            running = paired_matmul(rows[level], backward_stacks[level])
        return rows, running

    def backward_hop(_, running):
        return lax.ppermute(backward_levels(running)[1], "chain", odds)

    arriving = jnp.zeros((samples, level_rows), jnp.float32)
    arriving = lax.fori_loop(0, pair_count - 1, backward_hop, arriving, unroll=chain <= 8)
    arriving = jnp.where(is_odd, arriving, lax.ppermute(arriving, "chain", to_even))
    pending_rows, _ = backward_levels(arriving)

    forward_pair = jnp.stack([rows[:, :sup_rows] for rows in solved])
    pending_pair = jnp.stack([rows[:, :sup_rows] for rows in pending_rows])
    forward_own = jnp.where(is_odd, forward_pair[levels:], forward_pair[:levels])
    pending_own = jnp.where(is_odd, pending_pair[levels:], pending_pair[:levels])
    answers = jnp.stack([matmul(pending_own[level], inverse_diag[level, 0]) for level in range(levels)])
    return (forward_own[:, None], answers[:, None])


def solution(mesh):
    return jax.shard_map(
        shards,
        mesh=mesh,
        in_specs=(
            P("chain", "grp", None, None),
            P("chain", "grp", None, None, None),
            P("chain", "grp", None, None),
            P("chain", None, None),
        ),
        out_specs=(P("chain", "grp", None, None), P("chain", "grp", None, None)),
        check_vma=False,
    )
```

```python
import jax
import jax.numpy as jnp
from jax import lax
from jax.sharding import PartitionSpec as P

PRECISE = lax.Precision.HIGHEST


def matmul(left_side, right_factor):
    return jnp.dot(left_side, right_factor, precision=PRECISE, preferred_element_type=jnp.float32)


def matmul_trans(left_side, right_factor):
    return lax.dot_general(
        left_side,
        right_factor,
        (((1,), (1,)), ((), ())),
        precision=PRECISE,
        preferred_element_type=jnp.float32,
    )


TERMS = 3


def split_parts(value, count):
    parts = []
    rest = value
    for _ in range(count):
        part = rest.astype(jnp.bfloat16)
        parts.append(part)
        rest = rest - part.astype(jnp.float32)
    return parts


def term_pairs(count):
    return [(left, right) for left in range(count) for right in range(count) if left + right < count]


def stack_right(value, count):
    parts = split_parts(value, count)
    return jnp.concatenate([parts[right] for _, right in term_pairs(count)], axis=0)


def split_matmul(left_side, stacked):
    count = 2 if TERMS == 3 else 3
    parts = split_parts(left_side, count)
    stacked_left = jnp.concatenate([parts[left] for left, _ in term_pairs(count)], axis=1)
    return jnp.dot(stacked_left, stacked, preferred_element_type=jnp.float32)


def shards(right_side, factor, inverse_diag, pattern):
    levels = right_side.shape[0]
    samples = right_side.shape[2]
    sup_rows = right_side.shape[3]
    groups = lax.axis_size("grp")
    chain = lax.axis_size("chain")
    level_rows = groups * sup_rows
    my_group = lax.axis_index("grp")
    scaled = jnp.einsum(
        "lgti,lgkij->lgktj",
        inverse_diag,
        factor,
        precision=PRECISE,
        preferred_element_type=jnp.float32,
    )
    lifted = jnp.einsum(
        "lgsi,lgti->lgst",
        right_side,
        inverse_diag,
        precision=PRECISE,
        preferred_element_type=jnp.float32,
    )
    knb = factor.shape[2]
    block_size = knb * sup_rows
    my_chain = lax.axis_index("chain")
    is_odd = my_chain % 2 == 1
    packed = jnp.concatenate(
        [scaled.reshape(levels, block_size, sup_rows), lifted.reshape(levels, samples, sup_rows)], axis=1
    )
    own_pieces = [packed]
    for shift in range(1, groups):
        own_pieces.append(lax.ppermute(packed, "grp", [(h, (h + shift) % groups) for h in range(groups)]))
    partner_pieces = []
    for shift in range(groups):
        pairs = [
            (position * groups + h, (position ^ 1) * groups + (h + shift) % groups)
            for position in range(chain)
            for h in range(groups)
        ]
        partner_pieces.append(lax.ppermute(packed, ("chain", "grp"), pairs))
    swap = [(position, position ^ 1) for position in range(chain)]
    partner_pattern = lax.ppermute(pattern, "chain", swap)
    own_stacked = jnp.stack(own_pieces, axis=1)
    partner_stacked = jnp.stack(partner_pieces, axis=1)
    pair_stacked = jnp.concatenate(
        [jnp.where(is_odd, partner_stacked, own_stacked), jnp.where(is_odd, own_stacked, partner_stacked)], axis=0
    )
    pair_pattern = jnp.concatenate(
        [jnp.where(is_odd, partner_pattern, pattern), jnp.where(is_odd, pattern, partner_pattern)], axis=0
    )
    pair_levels = 2 * levels
    blocks = pair_stacked[:, :, :block_size].reshape(pair_levels, groups, knb, sup_rows, sup_rows)
    offsets = pair_stacked[:, :, block_size:]
    slot_group = (my_group - jnp.arange(groups, dtype=jnp.int32)) % groups
    pattern_slots = jnp.take(pair_pattern, slot_group, axis=1)
    onehot = (pattern_slots[..., None] == slot_group).astype(jnp.float32)
    coupling = jnp.einsum(
        "lgkh,lgktj->lgthj", onehot, blocks, precision=PRECISE, preferred_element_type=jnp.float32
    )
    coupling = coupling.reshape(pair_levels, level_rows, level_rows)
    sources = offsets.transpose(0, 2, 1, 3).reshape(pair_levels, samples, level_rows)

    count = 2 if TERMS == 3 else 3
    chosen_parts = []
    forward_stacks = []
    for level in range(pair_levels):
        chosen_parts.append(split_parts(coupling[level], 2))
        forward_stacks.append(jnp.concatenate(chosen_parts[-1], axis=1))

    def row_stacked(state):
        high, low = split_parts(state, 2)
        return jnp.concatenate(
            [jnp.concatenate([high, high], axis=1), jnp.concatenate([low, jnp.zeros_like(low)], axis=1)], axis=0
        )

    def paired_matmul(state, stacked):
        out = jnp.dot(row_stacked(state), stacked, preferred_element_type=jnp.float32)
        return out[:samples] + out[samples:]

    def forward_product(state, stacked):
        out = lax.dot_general(
            row_stacked(state), stacked, (((1,), (1,)), ((), ())), preferred_element_type=jnp.float32
        )
        return out[:samples] + out[samples:]

    def forward_levels(state):
        rows = []
        for level in range(pair_levels):
            state = sources[level] - forward_product(state, forward_stacks[level])
            rows.append(state)
        return rows

    pair_count = chain // 2
    evens = [(2 * pair, 2 * pair + 2) for pair in range(pair_count - 1)]
    odds = [(2 * pair + 3, 2 * pair + 1) for pair in range(pair_count - 1)]
    to_odd = [(2 * pair, 2 * pair + 1) for pair in range(pair_count)]
    to_even = [(2 * pair + 1, 2 * pair) for pair in range(pair_count)]

    def forward_hop(_, state):
        return lax.ppermute(forward_levels(state)[-1], "chain", evens)

    incoming = jnp.zeros((samples, level_rows), jnp.float32)
    if pair_count > 1:
        first_out = forward_levels(incoming)[-1]
        incoming = lax.ppermute(first_out, "chain", evens)
        chosen_parts, _ = lax.optimization_barrier((chosen_parts, first_out))
    backward_stacks = [jnp.concatenate(chosen, axis=0) for chosen in chosen_parts]
    incoming = lax.fori_loop(1, pair_count - 1, forward_hop, incoming, unroll=chain <= 8)
    incoming = jnp.where(is_odd, lax.ppermute(incoming, "chain", to_odd), incoming)
    solved = forward_levels(incoming)

    def backward_levels(running):
        rows = [None] * pair_levels
        for level in reversed(range(pair_levels)):
            rows[level] = solved[level] - running
            running = paired_matmul(rows[level], backward_stacks[level])
        return rows, running

    def backward_hop(_, running):
        return lax.ppermute(backward_levels(running)[1], "chain", odds)

    arriving = jnp.zeros((samples, level_rows), jnp.float32)
    arriving = lax.fori_loop(0, pair_count - 1, backward_hop, arriving, unroll=chain <= 8)
    arriving = jnp.where(is_odd, arriving, lax.ppermute(arriving, "chain", to_even))
    pending_rows, _ = backward_levels(arriving)

    forward_pair = jnp.stack([rows[:, :sup_rows] for rows in solved])
    pending_pair = jnp.stack([rows[:, :sup_rows] for rows in pending_rows])
    forward_own = jnp.where(is_odd, forward_pair[levels:], forward_pair[:levels])
    pending_own = jnp.where(is_odd, pending_pair[levels:], pending_pair[:levels])
    answers = jnp.stack([matmul(pending_own[level], inverse_diag[level, 0]) for level in range(levels)])
    return (forward_own[:, None], answers[:, None])


def solution(mesh):
    return jax.shard_map(
        shards,
        mesh=mesh,
        in_specs=(
            P("chain", "grp", None, None),
            P("chain", "grp", None, None, None),
            P("chain", "grp", None, None),
            P("chain", None, None),
        ),
        out_specs=(P("chain", "grp", None, None), P("chain", "grp", None, None)),
        check_vma=False,
    )
```

```python
import jax
import jax.numpy as jnp
from jax import lax
from jax.sharding import PartitionSpec as P

PRECISE = lax.Precision.HIGHEST


def matmul(left_side, right_factor):
    return jnp.dot(left_side, right_factor, precision=PRECISE, preferred_element_type=jnp.float32)


def matmul_trans(left_side, right_factor):
    return lax.dot_general(
        left_side,
        right_factor,
        (((1,), (1,)), ((), ())),
        precision=PRECISE,
        preferred_element_type=jnp.float32,
    )


TERMS = 3


def split_parts(value, count):
    parts = []
    rest = value
    for _ in range(count):
        part = rest.astype(jnp.bfloat16)
        parts.append(part)
        rest = rest - part.astype(jnp.float32)
    return parts


def term_pairs(count):
    return [(left, right) for left in range(count) for right in range(count) if left + right < count]


def stack_right(value, count):
    parts = split_parts(value, count)
    return jnp.concatenate([parts[right] for _, right in term_pairs(count)], axis=0)


def split_matmul(left_side, stacked):
    count = 2 if TERMS == 3 else 3
    parts = split_parts(left_side, count)
    stacked_left = jnp.concatenate([parts[left] for left, _ in term_pairs(count)], axis=1)
    return jnp.dot(stacked_left, stacked, preferred_element_type=jnp.float32)


def shards(right_side, factor, inverse_diag, pattern):
    levels = right_side.shape[0]
    samples = right_side.shape[2]
    sup_rows = right_side.shape[3]
    groups = lax.axis_size("grp")
    chain = lax.axis_size("chain")
    level_rows = groups * sup_rows
    my_group = lax.axis_index("grp")
    scaled = jnp.einsum(
        "lgti,lgkij->lgktj",
        inverse_diag,
        factor,
        precision=PRECISE,
        preferred_element_type=jnp.float32,
    )
    lifted = jnp.einsum(
        "lgsi,lgti->lgst",
        right_side,
        inverse_diag,
        precision=PRECISE,
        preferred_element_type=jnp.float32,
    )
    knb = factor.shape[2]
    block_size = knb * sup_rows
    my_chain = lax.axis_index("chain")
    is_odd = my_chain % 2 == 1
    packed = jnp.concatenate(
        [scaled.reshape(levels, block_size, sup_rows), lifted.reshape(levels, samples, sup_rows)], axis=1
    )
    own_pieces = [packed]
    for shift in range(1, groups):
        own_pieces.append(lax.ppermute(packed, "grp", [(h, (h + shift) % groups) for h in range(groups)]))
    partner_pieces = []
    for shift in range(groups):
        pairs = [
            (position * groups + h, (position ^ 1) * groups + (h + shift) % groups)
            for position in range(chain)
            for h in range(groups)
        ]
        partner_pieces.append(lax.ppermute(packed, ("chain", "grp"), pairs))
    swap = [(position, position ^ 1) for position in range(chain)]
    partner_pattern = lax.ppermute(pattern, "chain", swap)
    own_stacked = jnp.stack(own_pieces, axis=1)
    partner_stacked = jnp.stack(partner_pieces, axis=1)
    pair_stacked = jnp.concatenate(
        [jnp.where(is_odd, partner_stacked, own_stacked), jnp.where(is_odd, own_stacked, partner_stacked)], axis=0
    )
    pair_pattern = jnp.concatenate(
        [jnp.where(is_odd, partner_pattern, pattern), jnp.where(is_odd, pattern, partner_pattern)], axis=0
    )
    pair_levels = 2 * levels
    blocks = pair_stacked[:, :, :block_size].reshape(pair_levels, groups, knb, sup_rows, sup_rows)
    offsets = pair_stacked[:, :, block_size:]
    slot_group = (my_group - jnp.arange(groups, dtype=jnp.int32)) % groups
    pattern_slots = jnp.take(pair_pattern, slot_group, axis=1)
    onehot = (pattern_slots[..., None] == slot_group).astype(jnp.bfloat16)
    sources = offsets.transpose(0, 2, 1, 3).reshape(pair_levels, samples, level_rows)

    count = 2 if TERMS == 3 else 3
    coupling_parts = [
        jnp.einsum("lgkh,lgktj->lgthj", onehot, part, preferred_element_type=jnp.float32)
        .astype(jnp.bfloat16)
        .reshape(pair_levels, level_rows, level_rows)
        for part in split_parts(blocks, 2)
    ]
    chosen_parts = []
    forward_stacks = []
    for level in range(pair_levels):
        chosen_parts.append([part[level] for part in coupling_parts])
        forward_stacks.append(jnp.concatenate(chosen_parts[-1], axis=1))

    def row_stacked(state):
        high, low = split_parts(state, 2)
        return jnp.concatenate(
            [jnp.concatenate([high, high], axis=1), jnp.concatenate([low, jnp.zeros_like(low)], axis=1)], axis=0
        )

    def paired_matmul(state, stacked):
        out = jnp.dot(row_stacked(state), stacked, preferred_element_type=jnp.float32)
        return out[:samples] + out[samples:]

    def forward_product(state, stacked):
        out = lax.dot_general(
            row_stacked(state), stacked, (((1,), (1,)), ((), ())), preferred_element_type=jnp.float32
        )
        return out[:samples] + out[samples:]

    def forward_levels(state):
        rows = []
        for level in range(pair_levels):
            state = sources[level] - forward_product(state, forward_stacks[level])
            rows.append(state)
        return rows

    pair_count = chain // 2
    evens = [(2 * pair, 2 * pair + 2) for pair in range(pair_count - 1)]
    odds = [(2 * pair + 3, 2 * pair + 1) for pair in range(pair_count - 1)]
    to_odd = [(2 * pair, 2 * pair + 1) for pair in range(pair_count)]
    to_even = [(2 * pair + 1, 2 * pair) for pair in range(pair_count)]

    def forward_hop(_, state):
        return lax.ppermute(forward_levels(state)[-1], "chain", evens)

    incoming = jnp.zeros((samples, level_rows), jnp.float32)
    if pair_count > 1:
        first_out = forward_levels(incoming)[-1]
        incoming = lax.ppermute(first_out, "chain", evens)
        chosen_parts, _ = lax.optimization_barrier((chosen_parts, first_out))
    backward_stacks = [jnp.concatenate(chosen, axis=0) for chosen in chosen_parts]
    incoming = lax.fori_loop(1, pair_count - 1, forward_hop, incoming, unroll=chain <= 8)
    incoming = jnp.where(is_odd, lax.ppermute(incoming, "chain", to_odd), incoming)
    solved = forward_levels(incoming)

    def backward_levels(running):
        rows = [None] * pair_levels
        for level in reversed(range(pair_levels)):
            rows[level] = solved[level] - running
            running = paired_matmul(rows[level], backward_stacks[level])
        return rows, running

    def backward_hop(_, running):
        return lax.ppermute(backward_levels(running)[1], "chain", odds)

    arriving = jnp.zeros((samples, level_rows), jnp.float32)
    arriving = lax.fori_loop(0, pair_count - 1, backward_hop, arriving, unroll=chain <= 8)
    arriving = jnp.where(is_odd, arriving, lax.ppermute(arriving, "chain", to_even))
    pending_rows, _ = backward_levels(arriving)

    forward_pair = jnp.stack([rows[:, :sup_rows] for rows in solved])
    pending_pair = jnp.stack([rows[:, :sup_rows] for rows in pending_rows])
    forward_own = jnp.where(is_odd, forward_pair[levels:], forward_pair[:levels])
    pending_own = jnp.where(is_odd, pending_pair[levels:], pending_pair[:levels])
    answers = jnp.stack([matmul(pending_own[level], inverse_diag[level, 0]) for level in range(levels)])
    return (forward_own[:, None], answers[:, None])


def solution(mesh):
    return jax.shard_map(
        shards,
        mesh=mesh,
        in_specs=(
            P("chain", "grp", None, None),
            P("chain", "grp", None, None, None),
            P("chain", "grp", None, None),
            P("chain", None, None),
        ),
        out_specs=(P("chain", "grp", None, None), P("chain", "grp", None, None)),
        check_vma=False,
    )
```

```python
import jax
import jax.numpy as jnp
from jax import lax
from jax.sharding import PartitionSpec as P

PRECISE = lax.Precision.HIGHEST


def matmul(left_side, right_factor):
    return jnp.dot(left_side, right_factor, precision=PRECISE, preferred_element_type=jnp.float32)


def matmul_trans(left_side, right_factor):
    return lax.dot_general(
        left_side,
        right_factor,
        (((1,), (1,)), ((), ())),
        precision=PRECISE,
        preferred_element_type=jnp.float32,
    )


TERMS = 3


def split_parts(value, count):
    parts = []
    rest = value
    for _ in range(count):
        part = rest.astype(jnp.bfloat16)
        parts.append(part)
        rest = rest - part.astype(jnp.float32)
    return parts


def term_pairs(count):
    return [(left, right) for left in range(count) for right in range(count) if left + right < count]


def stack_right(value, count):
    parts = split_parts(value, count)
    return jnp.concatenate([parts[right] for _, right in term_pairs(count)], axis=0)


def split_matmul(left_side, stacked):
    count = 2 if TERMS == 3 else 3
    parts = split_parts(left_side, count)
    stacked_left = jnp.concatenate([parts[left] for left, _ in term_pairs(count)], axis=1)
    return jnp.dot(stacked_left, stacked, preferred_element_type=jnp.float32)


def shards(right_side, factor, inverse_diag, pattern):
    levels = right_side.shape[0]
    samples = right_side.shape[2]
    sup_rows = right_side.shape[3]
    groups = lax.axis_size("grp")
    chain = lax.axis_size("chain")
    level_rows = groups * sup_rows
    my_group = lax.axis_index("grp")
    scaled = jnp.einsum(
        "lgti,lgkij->lgktj",
        inverse_diag,
        factor,
        precision=PRECISE,
        preferred_element_type=jnp.float32,
    )
    lifted = jnp.einsum(
        "lgsi,lgti->lgst",
        right_side,
        inverse_diag,
        precision=PRECISE,
        preferred_element_type=jnp.float32,
    )
    knb = factor.shape[2]
    block_size = knb * sup_rows
    my_chain = lax.axis_index("chain")
    is_odd = my_chain % 2 == 1
    packed = jnp.concatenate(
        [scaled.reshape(levels, block_size, sup_rows), lifted.reshape(levels, samples, sup_rows)], axis=1
    )
    own_pieces = [packed]
    for shift in range(1, groups):
        own_pieces.append(lax.ppermute(packed, "grp", [(h, (h + shift) % groups) for h in range(groups)]))
    partner_pieces = []
    for shift in range(groups):
        pairs = [
            (position * groups + h, (position ^ 1) * groups + (h + shift) % groups)
            for position in range(chain)
            for h in range(groups)
        ]
        partner_pieces.append(lax.ppermute(packed, ("chain", "grp"), pairs))
    swap = [(position, position ^ 1) for position in range(chain)]
    partner_pattern = lax.ppermute(pattern, "chain", swap)
    own_stacked = jnp.stack(own_pieces, axis=1)
    partner_stacked = jnp.stack(partner_pieces, axis=1)
    pair_stacked = jnp.concatenate(
        [jnp.where(is_odd, partner_stacked, own_stacked), jnp.where(is_odd, own_stacked, partner_stacked)], axis=0
    )
    pair_pattern = jnp.concatenate(
        [jnp.where(is_odd, partner_pattern, pattern), jnp.where(is_odd, pattern, partner_pattern)], axis=0
    )
    pair_levels = 2 * levels
    blocks = pair_stacked[:, :, :block_size].reshape(pair_levels, groups, knb, sup_rows, sup_rows)
    offsets = pair_stacked[:, :, block_size:]
    slot_group = (my_group - jnp.arange(groups, dtype=jnp.int32)) % groups
    pattern_slots = jnp.take(pair_pattern, slot_group, axis=1)
    onehot = (pattern_slots[..., None] == slot_group).astype(jnp.float32)
    coupling = jnp.einsum(
        "lgkh,lgktj->lgthj", onehot, blocks, precision=PRECISE, preferred_element_type=jnp.float32
    )
    coupling = coupling.reshape(pair_levels, level_rows, level_rows)
    sources = offsets.transpose(0, 2, 1, 3).reshape(pair_levels, samples, level_rows)

    count = 2 if TERMS == 3 else 3
    chosen_parts = []
    forward_stacks = []
    for level in range(pair_levels):
        chosen_parts.append(split_parts(coupling[level], 2))
        forward_stacks.append(jnp.concatenate(chosen_parts[-1], axis=1))

    def row_stacked(state):
        high, low = split_parts(state, 2)
        return jnp.concatenate(
            [jnp.concatenate([high, high], axis=1), jnp.concatenate([low, jnp.zeros_like(low)], axis=1)], axis=0
        )

    def paired_matmul(state, stacked):
        out = jnp.dot(row_stacked(state), stacked, preferred_element_type=jnp.float32)
        return out[:samples] + out[samples:]

    def forward_product(state, stacked):
        out = lax.dot_general(
            row_stacked(state), stacked, (((1,), (1,)), ((), ())), preferred_element_type=jnp.float32
        )
        return out[:samples] + out[samples:]

    def forward_levels(state):
        rows = []
        for level in range(pair_levels):
            state = sources[level] - forward_product(state, forward_stacks[level])
            rows.append(state)
        return rows

    pair_count = chain // 2
    evens = [(2 * pair, 2 * pair + 2) for pair in range(pair_count - 1)]
    odds = [(2 * pair + 3, 2 * pair + 1) for pair in range(pair_count - 1)]
    to_odd = [(2 * pair, 2 * pair + 1) for pair in range(pair_count)]
    to_even = [(2 * pair + 1, 2 * pair) for pair in range(pair_count)]

    def forward_hop(_, state):
        return lax.ppermute(forward_levels(state)[-1], "chain", evens)

    incoming = jnp.zeros((samples, level_rows), jnp.float32)
    if pair_count > 1:
        first_out = forward_levels(incoming)[-1]
        incoming = lax.ppermute(first_out, "chain", evens)
        chosen_parts, _ = lax.optimization_barrier((chosen_parts, first_out))
    backward_stacks = [jnp.concatenate(chosen, axis=0) for chosen in chosen_parts]
    incoming = lax.fori_loop(1, pair_count - 1, forward_hop, incoming, unroll=chain <= 8)
    solved_here = forward_levels(incoming)
    incoming = jnp.where(is_odd, lax.ppermute(incoming, "chain", to_odd), incoming)
    solved = forward_levels(incoming)

    def backward_levels(running, states=None):
        states = solved if states is None else states
        rows = [None] * pair_levels
        for level in reversed(range(pair_levels)):
            rows[level] = states[level] - running
            running = paired_matmul(rows[level], backward_stacks[level])
        return rows, running

    inner_odds = [(2 * pair + 3, 2 * pair + 1) for pair in range(pair_count - 2)]

    def backward_hop(_, running):
        passed = lax.ppermute(backward_levels(running)[1], "chain", inner_odds)
        return jnp.where(my_chain >= chain - 3, running, passed)

    arriving = jnp.zeros((samples, level_rows), jnp.float32)
    if pair_count > 1:
        first_back = backward_levels(arriving, solved_here)[1]
        arriving = lax.ppermute(first_back, "chain", [(chain - 2, chain - 3)])
    arriving = lax.fori_loop(0, max(pair_count - 2, 0), backward_hop, arriving, unroll=chain <= 8)
    arriving = jnp.where(is_odd, arriving, lax.ppermute(arriving, "chain", to_even[:-1]))
    pending_rows, _ = backward_levels(arriving)

    forward_pair = jnp.stack([rows[:, :sup_rows] for rows in solved])
    pending_pair = jnp.stack([rows[:, :sup_rows] for rows in pending_rows])
    forward_own = jnp.where(is_odd, forward_pair[levels:], forward_pair[:levels])
    pending_own = jnp.where(is_odd, pending_pair[levels:], pending_pair[:levels])
    answers = jnp.stack([matmul(pending_own[level], inverse_diag[level, 0]) for level in range(levels)])
    return (forward_own[:, None], answers[:, None])


def solution(mesh):
    return jax.shard_map(
        shards,
        mesh=mesh,
        in_specs=(
            P("chain", "grp", None, None),
            P("chain", "grp", None, None, None),
            P("chain", "grp", None, None),
            P("chain", None, None),
        ),
        out_specs=(P("chain", "grp", None, None), P("chain", "grp", None, None)),
        check_vma=False,
    )
```

```python
import jax
import jax.numpy as jnp
from jax import lax
from jax.sharding import PartitionSpec as P

PRECISE = lax.Precision.HIGHEST


def matmul(left_side, right_factor):
    return jnp.dot(left_side, right_factor, precision=PRECISE, preferred_element_type=jnp.float32)


def matmul_trans(left_side, right_factor):
    return lax.dot_general(
        left_side,
        right_factor,
        (((1,), (1,)), ((), ())),
        precision=PRECISE,
        preferred_element_type=jnp.float32,
    )


TERMS = 3


def split_parts(value, count):
    parts = []
    rest = value
    for _ in range(count):
        part = rest.astype(jnp.bfloat16)
        parts.append(part)
        rest = rest - part.astype(jnp.float32)
    return parts


def term_pairs(count):
    return [(left, right) for left in range(count) for right in range(count) if left + right < count]


def stack_right(value, count):
    parts = split_parts(value, count)
    return jnp.concatenate([parts[right] for _, right in term_pairs(count)], axis=0)


def split_matmul(left_side, stacked):
    count = 2 if TERMS == 3 else 3
    parts = split_parts(left_side, count)
    stacked_left = jnp.concatenate([parts[left] for left, _ in term_pairs(count)], axis=1)
    return jnp.dot(stacked_left, stacked, preferred_element_type=jnp.float32)


def shards(right_side, factor, inverse_diag, pattern):
    levels = right_side.shape[0]
    samples = right_side.shape[2]
    sup_rows = right_side.shape[3]
    groups = lax.axis_size("grp")
    chain = lax.axis_size("chain")
    level_rows = groups * sup_rows
    my_group = lax.axis_index("grp")
    scaled = jnp.einsum(
        "lgti,lgkij->lgktj",
        inverse_diag,
        factor,
        precision=PRECISE,
        preferred_element_type=jnp.float32,
    )
    lifted = jnp.einsum(
        "lgsi,lgti->lgst",
        right_side,
        inverse_diag,
        precision=PRECISE,
        preferred_element_type=jnp.float32,
    )
    knb = factor.shape[2]
    block_size = knb * sup_rows
    my_chain = lax.axis_index("chain")
    is_odd = my_chain % 2 == 1
    packed = jnp.concatenate(
        [scaled.reshape(levels, block_size, sup_rows), lifted.reshape(levels, samples, sup_rows)], axis=1
    )
    own_pieces = [packed]
    for shift in range(1, groups):
        own_pieces.append(lax.ppermute(packed, "grp", [(h, (h + shift) % groups) for h in range(groups)]))
    partner_pieces = []
    for shift in range(groups):
        pairs = [
            (position * groups + h, (position ^ 1) * groups + (h + shift) % groups)
            for position in range(chain)
            for h in range(groups)
        ]
        partner_pieces.append(lax.ppermute(packed, ("chain", "grp"), pairs))
    swap = [(position, position ^ 1) for position in range(chain)]
    partner_pattern = lax.ppermute(pattern, "chain", swap)
    own_stacked = jnp.stack(own_pieces, axis=1)
    partner_stacked = jnp.stack(partner_pieces, axis=1)
    pair_stacked = jnp.concatenate(
        [jnp.where(is_odd, partner_stacked, own_stacked), jnp.where(is_odd, own_stacked, partner_stacked)], axis=0
    )
    pair_pattern = jnp.concatenate(
        [jnp.where(is_odd, partner_pattern, pattern), jnp.where(is_odd, pattern, partner_pattern)], axis=0
    )
    pair_levels = 2 * levels
    blocks = pair_stacked[:, :, :block_size].reshape(pair_levels, groups, knb, sup_rows, sup_rows)
    offsets = pair_stacked[:, :, block_size:]
    slot_group = (my_group - jnp.arange(groups, dtype=jnp.int32)) % groups
    pattern_slots = jnp.take(pair_pattern, slot_group, axis=1)
    onehot = (pattern_slots[..., None] == slot_group).astype(jnp.float32)
    coupling = jnp.einsum(
        "lgkh,lgktj->lgthj", onehot, blocks, precision=PRECISE, preferred_element_type=jnp.float32
    )
    coupling = coupling.reshape(pair_levels, level_rows, level_rows)
    sources = offsets.transpose(0, 2, 1, 3).reshape(pair_levels, samples, level_rows)

    count = 2 if TERMS == 3 else 3
    chosen_parts = []
    forward_stacks = []
    for level in range(pair_levels):
        chosen_parts.append(split_parts(coupling[level], 2))
        forward_stacks.append(jnp.concatenate(chosen_parts[-1], axis=1))

    def row_stacked(state):
        high, low = split_parts(state, 2)
        return jnp.concatenate(
            [jnp.concatenate([high, high], axis=1), jnp.concatenate([low, jnp.zeros_like(low)], axis=1)], axis=0
        )

    def paired_matmul(state, stacked):
        out = jnp.dot(row_stacked(state), stacked, preferred_element_type=jnp.float32)
        return out[:samples] + out[samples:]

    def forward_product(state, stacked):
        out = lax.dot_general(
            row_stacked(state), stacked, (((1,), (1,)), ((), ())), preferred_element_type=jnp.float32
        )
        return out[:samples] + out[samples:]

    def forward_levels(state):
        rows = []
        for level in range(pair_levels):
            state = sources[level] - forward_product(state, forward_stacks[level])
            rows.append(state)
        return rows

    pair_count = chain // 2
    evens = [(2 * pair, 2 * pair + 2) for pair in range(pair_count - 1)]
    odds = [(2 * pair + 3, 2 * pair + 1) for pair in range(pair_count - 1)]
    to_odd = [(2 * pair, 2 * pair + 1) for pair in range(pair_count)]
    to_even = [(2 * pair + 1, 2 * pair) for pair in range(pair_count)]

    def forward_hop(_, state):
        return lax.ppermute(forward_levels(state)[-1], "chain", evens)

    incoming = jnp.zeros((samples, level_rows), jnp.float32)
    if pair_count > 1:
        first_out = forward_levels(incoming)[-1]
        incoming = lax.ppermute(first_out, "chain", evens)
        chosen_parts, _ = lax.optimization_barrier((chosen_parts, first_out))
    backward_stacks = [jnp.concatenate(chosen, axis=0) for chosen in chosen_parts]
    incoming = lax.fori_loop(1, pair_count - 1, forward_hop, incoming, unroll=chain <= 8)
    def backward_run(running, states):
        for level in reversed(range(pair_levels)):
            running = paired_matmul(states[level] - running, backward_stacks[level])
        return running

    solved_here = forward_levels(incoming)
    zeros = jnp.zeros((samples, level_rows), jnp.float32)
    first_back = zeros
    if pair_count > 1:
        first_back = backward_run(zeros, solved_here)
        incoming, first_back = lax.optimization_barrier((incoming, first_back))
    incoming = jnp.where(is_odd, lax.ppermute(incoming, "chain", to_odd), incoming)
    solved = forward_levels(incoming)

    def backward_levels(running, states=None):
        states = solved if states is None else states
        rows = [None] * pair_levels
        for level in reversed(range(pair_levels)):
            rows[level] = states[level] - running
            running = paired_matmul(rows[level], backward_stacks[level])
        return rows, running

    inner_odds = [(2 * pair + 3, 2 * pair + 1) for pair in range(pair_count - 2)]

    def backward_hop(_, running):
        passed = lax.ppermute(backward_levels(running)[1], "chain", inner_odds)
        return jnp.where(my_chain >= chain - 3, running, passed)

    arriving = zeros
    if pair_count > 1:
        arriving = lax.ppermute(first_back, "chain", [(chain - 2, chain - 3)])
    arriving = lax.fori_loop(0, max(pair_count - 2, 0), backward_hop, arriving, unroll=chain <= 8)
    arriving = jnp.where(is_odd, arriving, lax.ppermute(arriving, "chain", to_even[:-1]))
    pending_rows, _ = backward_levels(arriving)

    forward_pair = jnp.stack([rows[:, :sup_rows] for rows in solved])
    pending_pair = jnp.stack([rows[:, :sup_rows] for rows in pending_rows])
    forward_own = jnp.where(is_odd, forward_pair[levels:], forward_pair[:levels])
    pending_own = jnp.where(is_odd, pending_pair[levels:], pending_pair[:levels])
    answers = jnp.stack([matmul(pending_own[level], inverse_diag[level, 0]) for level in range(levels)])
    return (forward_own[:, None], answers[:, None])


def solution(mesh):
    return jax.shard_map(
        shards,
        mesh=mesh,
        in_specs=(
            P("chain", "grp", None, None),
            P("chain", "grp", None, None, None),
            P("chain", "grp", None, None),
            P("chain", None, None),
        ),
        out_specs=(P("chain", "grp", None, None), P("chain", "grp", None, None)),
        check_vma=False,
    )
```

```python
import jax
import jax.numpy as jnp
from jax import lax
from jax.sharding import PartitionSpec as P

PRECISE = lax.Precision.HIGHEST


def matmul(left_side, right_factor):
    return jnp.dot(left_side, right_factor, precision=PRECISE, preferred_element_type=jnp.float32)


def matmul_trans(left_side, right_factor):
    return lax.dot_general(
        left_side,
        right_factor,
        (((1,), (1,)), ((), ())),
        precision=PRECISE,
        preferred_element_type=jnp.float32,
    )


TERMS = 3


def split_parts(value, count):
    parts = []
    rest = value
    for _ in range(count):
        part = rest.astype(jnp.bfloat16)
        parts.append(part)
        rest = rest - part.astype(jnp.float32)
    return parts


def term_pairs(count):
    return [(left, right) for left in range(count) for right in range(count) if left + right < count]


def stack_right(value, count):
    parts = split_parts(value, count)
    return jnp.concatenate([parts[right] for _, right in term_pairs(count)], axis=0)


def split_matmul(left_side, stacked):
    count = 2 if TERMS == 3 else 3
    parts = split_parts(left_side, count)
    stacked_left = jnp.concatenate([parts[left] for left, _ in term_pairs(count)], axis=1)
    return jnp.dot(stacked_left, stacked, preferred_element_type=jnp.float32)


def shards(right_side, factor, inverse_diag, pattern):
    levels = right_side.shape[0]
    samples = right_side.shape[2]
    sup_rows = right_side.shape[3]
    groups = lax.axis_size("grp")
    chain = lax.axis_size("chain")
    level_rows = groups * sup_rows
    my_group = lax.axis_index("grp")
    scaled = jnp.einsum(
        "lgti,lgkij->lgktj",
        inverse_diag,
        factor,
        precision=lax.Precision.HIGH,
        preferred_element_type=jnp.float32,
    )
    lifted = jnp.einsum(
        "lgsi,lgti->lgst",
        right_side,
        inverse_diag,
        precision=lax.Precision.HIGH,
        preferred_element_type=jnp.float32,
    )
    knb = factor.shape[2]
    block_size = knb * sup_rows
    my_chain = lax.axis_index("chain")
    is_odd = my_chain % 2 == 1
    packed = jnp.concatenate(
        [scaled.reshape(levels, block_size, sup_rows), lifted.reshape(levels, samples, sup_rows)], axis=1
    )
    own_pieces = [packed]
    for shift in range(1, groups):
        own_pieces.append(lax.ppermute(packed, "grp", [(h, (h + shift) % groups) for h in range(groups)]))
    partner_pieces = []
    for shift in range(groups):
        pairs = [
            (position * groups + h, (position ^ 1) * groups + (h + shift) % groups)
            for position in range(chain)
            for h in range(groups)
        ]
        partner_pieces.append(lax.ppermute(packed, ("chain", "grp"), pairs))
    swap = [(position, position ^ 1) for position in range(chain)]
    partner_pattern = lax.ppermute(pattern, "chain", swap)
    own_stacked = jnp.stack(own_pieces, axis=1)
    partner_stacked = jnp.stack(partner_pieces, axis=1)
    pair_stacked = jnp.concatenate(
        [jnp.where(is_odd, partner_stacked, own_stacked), jnp.where(is_odd, own_stacked, partner_stacked)], axis=0
    )
    pair_pattern = jnp.concatenate(
        [jnp.where(is_odd, partner_pattern, pattern), jnp.where(is_odd, pattern, partner_pattern)], axis=0
    )
    pair_levels = 2 * levels
    blocks = pair_stacked[:, :, :block_size].reshape(pair_levels, groups, knb, sup_rows, sup_rows)
    offsets = pair_stacked[:, :, block_size:]
    slot_group = (my_group - jnp.arange(groups, dtype=jnp.int32)) % groups
    pattern_slots = jnp.take(pair_pattern, slot_group, axis=1)
    onehot = (pattern_slots[..., None] == slot_group).astype(jnp.float32)
    coupling = jnp.einsum(
        "lgkh,lgktj->lgthj", onehot, blocks, precision=PRECISE, preferred_element_type=jnp.float32
    )
    coupling = coupling.reshape(pair_levels, level_rows, level_rows)
    sources = offsets.transpose(0, 2, 1, 3).reshape(pair_levels, samples, level_rows)

    count = 2 if TERMS == 3 else 3
    chosen_parts = []
    forward_stacks = []
    for level in range(pair_levels):
        chosen_parts.append(split_parts(coupling[level], 2))
        forward_stacks.append(jnp.concatenate(chosen_parts[-1], axis=1))

    def row_stacked(state):
        high, low = split_parts(state, 2)
        return jnp.concatenate(
            [jnp.concatenate([high, high], axis=1), jnp.concatenate([low, jnp.zeros_like(low)], axis=1)], axis=0
        )

    def paired_matmul(state, stacked):
        out = jnp.dot(row_stacked(state), stacked, preferred_element_type=jnp.float32)
        return out[:samples] + out[samples:]

    def forward_product(state, stacked):
        out = lax.dot_general(
            row_stacked(state), stacked, (((1,), (1,)), ((), ())), preferred_element_type=jnp.float32
        )
        return out[:samples] + out[samples:]

    def forward_levels(state):
        rows = []
        for level in range(pair_levels):
            state = sources[level] - forward_product(state, forward_stacks[level])
            rows.append(state)
        return rows

    pair_count = chain // 2
    evens = [(2 * pair, 2 * pair + 2) for pair in range(pair_count - 1)]
    odds = [(2 * pair + 3, 2 * pair + 1) for pair in range(pair_count - 1)]
    to_odd = [(2 * pair, 2 * pair + 1) for pair in range(pair_count)]
    to_even = [(2 * pair + 1, 2 * pair) for pair in range(pair_count)]

    def forward_hop(_, state):
        return lax.ppermute(forward_levels(state)[-1], "chain", evens)

    incoming = jnp.zeros((samples, level_rows), jnp.float32)
    if pair_count > 1:
        first_out = forward_levels(incoming)[-1]
        incoming = lax.ppermute(first_out, "chain", evens)
        chosen_parts, _ = lax.optimization_barrier((chosen_parts, first_out))
    backward_stacks = [jnp.concatenate(chosen, axis=0) for chosen in chosen_parts]
    incoming = lax.fori_loop(1, pair_count - 1, forward_hop, incoming, unroll=chain <= 8)
    incoming = jnp.where(is_odd, lax.ppermute(incoming, "chain", to_odd), incoming)
    solved = forward_levels(incoming)

    def backward_levels(running):
        rows = [None] * pair_levels
        for level in reversed(range(pair_levels)):
            rows[level] = solved[level] - running
            running = paired_matmul(rows[level], backward_stacks[level])
        return rows, running

    def backward_hop(_, running):
        return lax.ppermute(backward_levels(running)[1], "chain", odds)

    arriving = jnp.zeros((samples, level_rows), jnp.float32)
    arriving = lax.fori_loop(0, pair_count - 1, backward_hop, arriving, unroll=chain <= 8)
    arriving = jnp.where(is_odd, arriving, lax.ppermute(arriving, "chain", to_even))
    pending_rows, _ = backward_levels(arriving)

    forward_pair = jnp.stack([rows[:, :sup_rows] for rows in solved])
    pending_pair = jnp.stack([rows[:, :sup_rows] for rows in pending_rows])
    forward_own = jnp.where(is_odd, forward_pair[levels:], forward_pair[:levels])
    pending_own = jnp.where(is_odd, pending_pair[levels:], pending_pair[:levels])
    answers = jnp.stack([matmul(pending_own[level], inverse_diag[level, 0]) for level in range(levels)])
    return (forward_own[:, None], answers[:, None])


def solution(mesh):
    return jax.shard_map(
        shards,
        mesh=mesh,
        in_specs=(
            P("chain", "grp", None, None),
            P("chain", "grp", None, None, None),
            P("chain", "grp", None, None),
            P("chain", None, None),
        ),
        out_specs=(P("chain", "grp", None, None), P("chain", "grp", None, None)),
        check_vma=False,
    )
```

```python
import jax
import jax.numpy as jnp
from jax import lax
from jax.sharding import PartitionSpec as P

PRECISE = lax.Precision.HIGHEST


def matmul(left_side, right_factor):
    return jnp.dot(left_side, right_factor, precision=PRECISE, preferred_element_type=jnp.float32)


def matmul_trans(left_side, right_factor):
    return lax.dot_general(
        left_side,
        right_factor,
        (((1,), (1,)), ((), ())),
        precision=PRECISE,
        preferred_element_type=jnp.float32,
    )


TERMS = 3


def split_parts(value, count):
    parts = []
    rest = value
    for _ in range(count):
        part = rest.astype(jnp.bfloat16)
        parts.append(part)
        rest = rest - part.astype(jnp.float32)
    return parts


def term_pairs(count):
    return [(left, right) for left in range(count) for right in range(count) if left + right < count]


def stack_right(value, count):
    parts = split_parts(value, count)
    return jnp.concatenate([parts[right] for _, right in term_pairs(count)], axis=0)


def split_matmul(left_side, stacked):
    count = 2 if TERMS == 3 else 3
    parts = split_parts(left_side, count)
    stacked_left = jnp.concatenate([parts[left] for left, _ in term_pairs(count)], axis=1)
    return jnp.dot(stacked_left, stacked, preferred_element_type=jnp.float32)


def shards(right_side, factor, inverse_diag, pattern):
    levels = right_side.shape[0]
    samples = right_side.shape[2]
    sup_rows = right_side.shape[3]
    groups = lax.axis_size("grp")
    chain = lax.axis_size("chain")
    level_rows = groups * sup_rows
    my_group = lax.axis_index("grp")
    scaled = jnp.einsum(
        "lgti,lgkij->lgktj",
        inverse_diag,
        factor,
        precision=PRECISE,
        preferred_element_type=jnp.float32,
    )
    lifted = jnp.einsum(
        "lgsi,lgti->lgst",
        right_side,
        inverse_diag,
        precision=PRECISE,
        preferred_element_type=jnp.float32,
    )
    knb = factor.shape[2]
    block_size = knb * sup_rows
    my_chain = lax.axis_index("chain")
    is_odd = my_chain % 2 == 1
    pattern_rows = jnp.zeros((levels, 8, sup_rows), jnp.float32)
    pattern_rows = pattern_rows.at[:, 0, : groups * knb].set(pattern.reshape(levels, -1).astype(jnp.float32))
    packed = jnp.concatenate(
        [scaled.reshape(levels, block_size, sup_rows), lifted.reshape(levels, samples, sup_rows), pattern_rows],
        axis=1,
    )
    own_pieces = [packed]
    for shift in range(1, groups):
        own_pieces.append(lax.ppermute(packed, "grp", [(h, (h + shift) % groups) for h in range(groups)]))
    partner_pieces = []
    for shift in range(groups):
        pairs = [
            (position * groups + h, (position ^ 1) * groups + (h + shift) % groups)
            for position in range(chain)
            for h in range(groups)
        ]
        partner_pieces.append(lax.ppermute(packed, ("chain", "grp"), pairs))
    swap = [(position, position ^ 1) for position in range(chain)]
    partner_pattern = partner_pieces[0][:, block_size + samples, : groups * knb]
    partner_pattern = partner_pattern.astype(jnp.int32).reshape(pattern.shape)
    own_stacked = jnp.stack(own_pieces, axis=1)
    partner_stacked = jnp.stack(partner_pieces, axis=1)
    pair_stacked = jnp.concatenate(
        [jnp.where(is_odd, partner_stacked, own_stacked), jnp.where(is_odd, own_stacked, partner_stacked)], axis=0
    )
    pair_pattern = jnp.concatenate(
        [jnp.where(is_odd, partner_pattern, pattern), jnp.where(is_odd, pattern, partner_pattern)], axis=0
    )
    pair_levels = 2 * levels
    blocks = pair_stacked[:, :, :block_size].reshape(pair_levels, groups, knb, sup_rows, sup_rows)
    offsets = pair_stacked[:, :, block_size : block_size + samples]
    slot_group = (my_group - jnp.arange(groups, dtype=jnp.int32)) % groups
    pattern_slots = jnp.take(pair_pattern, slot_group, axis=1)
    onehot = (pattern_slots[..., None] == slot_group).astype(jnp.float32)
    coupling = jnp.einsum(
        "lgkh,lgktj->lgthj", onehot, blocks, precision=PRECISE, preferred_element_type=jnp.float32
    )
    coupling = coupling.reshape(pair_levels, level_rows, level_rows)
    sources = offsets.transpose(0, 2, 1, 3).reshape(pair_levels, samples, level_rows)

    count = 2 if TERMS == 3 else 3
    chosen_parts = []
    forward_stacks = []
    for level in range(pair_levels):
        chosen_parts.append(split_parts(coupling[level], 2))
        forward_stacks.append(jnp.concatenate(chosen_parts[-1], axis=1))

    def row_stacked(state):
        high, low = split_parts(state, 2)
        return jnp.concatenate(
            [jnp.concatenate([high, high], axis=1), jnp.concatenate([low, jnp.zeros_like(low)], axis=1)], axis=0
        )

    def paired_matmul(state, stacked):
        out = jnp.dot(row_stacked(state), stacked, preferred_element_type=jnp.float32)
        return out[:samples] + out[samples:]

    def forward_product(state, stacked):
        out = lax.dot_general(
            row_stacked(state), stacked, (((1,), (1,)), ((), ())), preferred_element_type=jnp.float32
        )
        return out[:samples] + out[samples:]

    def forward_levels(state):
        rows = []
        for level in range(pair_levels):
            state = sources[level] - forward_product(state, forward_stacks[level])
            rows.append(state)
        return rows

    pair_count = chain // 2
    evens = [(2 * pair, 2 * pair + 2) for pair in range(pair_count - 1)]
    odds = [(2 * pair + 3, 2 * pair + 1) for pair in range(pair_count - 1)]
    to_odd = [(2 * pair, 2 * pair + 1) for pair in range(pair_count)]
    to_even = [(2 * pair + 1, 2 * pair) for pair in range(pair_count)]

    def forward_hop(_, state):
        return lax.ppermute(forward_levels(state)[-1], "chain", evens)

    incoming = jnp.zeros((samples, level_rows), jnp.float32)
    if pair_count > 1:
        first_out = forward_levels(incoming)[-1]
        incoming = lax.ppermute(first_out, "chain", evens)
        chosen_parts, _ = lax.optimization_barrier((chosen_parts, first_out))
    backward_stacks = [jnp.concatenate(chosen, axis=0) for chosen in chosen_parts]
    incoming = lax.fori_loop(1, pair_count - 1, forward_hop, incoming, unroll=chain <= 8)
    incoming = jnp.where(is_odd, lax.ppermute(incoming, "chain", to_odd), incoming)
    solved = forward_levels(incoming)

    def backward_levels(running):
        rows = [None] * pair_levels
        for level in reversed(range(pair_levels)):
            rows[level] = solved[level] - running
            running = paired_matmul(rows[level], backward_stacks[level])
        return rows, running

    def backward_hop(_, running):
        return lax.ppermute(backward_levels(running)[1], "chain", odds)

    arriving = jnp.zeros((samples, level_rows), jnp.float32)
    arriving = lax.fori_loop(0, pair_count - 1, backward_hop, arriving, unroll=chain <= 8)
    arriving = jnp.where(is_odd, arriving, lax.ppermute(arriving, "chain", to_even))
    pending_rows, _ = backward_levels(arriving)

    forward_pair = jnp.stack([rows[:, :sup_rows] for rows in solved])
    pending_pair = jnp.stack([rows[:, :sup_rows] for rows in pending_rows])
    forward_own = jnp.where(is_odd, forward_pair[levels:], forward_pair[:levels])
    pending_own = jnp.where(is_odd, pending_pair[levels:], pending_pair[:levels])
    answers = jnp.stack([matmul(pending_own[level], inverse_diag[level, 0]) for level in range(levels)])
    return (forward_own[:, None], answers[:, None])


def solution(mesh):
    return jax.shard_map(
        shards,
        mesh=mesh,
        in_specs=(
            P("chain", "grp", None, None),
            P("chain", "grp", None, None, None),
            P("chain", "grp", None, None),
            P("chain", None, None),
        ),
        out_specs=(P("chain", "grp", None, None), P("chain", "grp", None, None)),
        check_vma=False,
    )
```

```python
import jax
import jax.numpy as jnp
from jax import lax
from jax.sharding import PartitionSpec as P

PRECISE = lax.Precision.HIGHEST


def matmul(left_side, right_factor):
    return jnp.dot(left_side, right_factor, precision=PRECISE, preferred_element_type=jnp.float32)


def matmul_trans(left_side, right_factor):
    return lax.dot_general(
        left_side,
        right_factor,
        (((1,), (1,)), ((), ())),
        precision=PRECISE,
        preferred_element_type=jnp.float32,
    )


TERMS = 3


def split_parts(value, count):
    parts = []
    rest = value
    for _ in range(count):
        part = rest.astype(jnp.bfloat16)
        parts.append(part)
        rest = rest - part.astype(jnp.float32)
    return parts


def term_pairs(count):
    return [(left, right) for left in range(count) for right in range(count) if left + right < count]


def stack_right(value, count):
    parts = split_parts(value, count)
    return jnp.concatenate([parts[right] for _, right in term_pairs(count)], axis=0)


def split_matmul(left_side, stacked):
    count = 2 if TERMS == 3 else 3
    parts = split_parts(left_side, count)
    stacked_left = jnp.concatenate([parts[left] for left, _ in term_pairs(count)], axis=1)
    return jnp.dot(stacked_left, stacked, preferred_element_type=jnp.float32)


def shards(right_side, factor, inverse_diag, pattern):
    levels = right_side.shape[0]
    samples = right_side.shape[2]
    sup_rows = right_side.shape[3]
    groups = lax.axis_size("grp")
    chain = lax.axis_size("chain")
    level_rows = groups * sup_rows
    my_group = lax.axis_index("grp")
    scaled = jnp.einsum(
        "lgti,lgkij->lgktj",
        inverse_diag,
        factor,
        precision=PRECISE,
        preferred_element_type=jnp.float32,
    )
    lifted = jnp.einsum(
        "lgsi,lgti->lgst",
        right_side,
        inverse_diag,
        precision=PRECISE,
        preferred_element_type=jnp.float32,
    )
    knb = factor.shape[2]
    block_size = knb * sup_rows
    my_chain = lax.axis_index("chain")
    is_odd = my_chain % 2 == 1
    packed = jnp.concatenate(
        [scaled.reshape(levels, block_size, sup_rows), lifted.reshape(levels, samples, sup_rows)], axis=1
    )
    own_pieces = [packed]
    for shift in range(1, groups):
        own_pieces.append(lax.ppermute(packed, "grp", [(h, (h + shift) % groups) for h in range(groups)]))
    partner_pieces = []
    for shift in range(groups):
        pairs = [
            (position * groups + h, (position ^ 1) * groups + (h + shift) % groups)
            for position in range(chain)
            for h in range(groups)
        ]
        partner_pieces.append(lax.ppermute(packed, ("chain", "grp"), pairs))
    swap = [(position, position ^ 1) for position in range(chain)]
    partner_pattern = lax.ppermute(pattern, "chain", swap)
    own_stacked = jnp.stack(own_pieces, axis=1)
    partner_stacked = jnp.stack(partner_pieces, axis=1)
    pair_stacked = jnp.concatenate(
        [jnp.where(is_odd, partner_stacked, own_stacked), jnp.where(is_odd, own_stacked, partner_stacked)], axis=0
    )
    pair_pattern = jnp.concatenate(
        [jnp.where(is_odd, partner_pattern, pattern), jnp.where(is_odd, pattern, partner_pattern)], axis=0
    )
    pair_levels = 2 * levels
    blocks = pair_stacked[:, :, :block_size].reshape(pair_levels, groups, knb, sup_rows, sup_rows)
    offsets = pair_stacked[:, :, block_size:]
    slot_group = (my_group - jnp.arange(groups, dtype=jnp.int32)) % groups
    pattern_slots = jnp.take(pair_pattern, slot_group, axis=1)
    onehot = (pattern_slots[..., None] == slot_group).astype(jnp.float32)
    coupling = jnp.einsum(
        "lgkh,lgktj->lgthj", onehot, blocks, precision=PRECISE, preferred_element_type=jnp.float32
    )
    coupling = coupling.reshape(pair_levels, level_rows, level_rows)
    sources = offsets.transpose(0, 2, 1, 3).reshape(pair_levels, samples, level_rows)

    count = 2 if TERMS == 3 else 3
    chosen_parts = []
    forward_stacks = []
    for level in range(pair_levels):
        chosen_parts.append(split_parts(coupling[level], 2))
        forward_stacks.append(jnp.concatenate(chosen_parts[-1], axis=1))

    def row_stacked(state):
        high, low = split_parts(state, 2)
        return jnp.concatenate(
            [jnp.concatenate([high, high], axis=1), jnp.concatenate([low, jnp.zeros_like(low)], axis=1)], axis=0
        )

    def paired_matmul(state, stacked):
        out = jnp.dot(row_stacked(state), stacked, preferred_element_type=jnp.float32)
        return out[:samples] + out[samples:]

    def forward_product(state, stacked):
        out = lax.dot_general(
            row_stacked(state), stacked, (((1,), (1,)), ((), ())), preferred_element_type=jnp.float32
        )
        return out[:samples] + out[samples:]

    def forward_levels(state, start=0):
        rows = []
        for level in range(start, pair_levels):
            state = sources[level] - forward_product(state, forward_stacks[level])
            rows.append(state)
        return rows

    pair_count = chain // 2
    evens = [(2 * pair, 2 * pair + 2) for pair in range(pair_count - 1)]
    odds = [(2 * pair + 3, 2 * pair + 1) for pair in range(pair_count - 1)]
    to_odd = [(2 * pair, 2 * pair + 1) for pair in range(pair_count)]
    to_even = [(2 * pair + 1, 2 * pair) for pair in range(pair_count)]

    def forward_hop(_, state):
        return lax.ppermute(forward_levels(state)[-1], "chain", evens)

    incoming = jnp.zeros((samples, level_rows), jnp.float32)
    if pair_count > 1:
        first_out = forward_levels(sources[0], 1)[-1] if pair_levels > 1 else sources[0]
        incoming = lax.ppermute(first_out, "chain", evens)
        chosen_parts, _ = lax.optimization_barrier((chosen_parts, first_out))
    backward_stacks = [jnp.concatenate(chosen, axis=0) for chosen in chosen_parts]
    incoming = lax.fori_loop(1, pair_count - 1, forward_hop, incoming, unroll=chain <= 8)
    incoming = jnp.where(is_odd, lax.ppermute(incoming, "chain", to_odd), incoming)
    solved = forward_levels(incoming)

    def backward_levels(running):
        rows = [None] * pair_levels
        for level in reversed(range(pair_levels)):
            rows[level] = solved[level] - running
            running = paired_matmul(rows[level], backward_stacks[level])
        return rows, running

    def backward_hop(_, running):
        return lax.ppermute(backward_levels(running)[1], "chain", odds)

    arriving = jnp.zeros((samples, level_rows), jnp.float32)
    arriving = lax.fori_loop(0, pair_count - 1, backward_hop, arriving, unroll=chain <= 8)
    arriving = jnp.where(is_odd, arriving, lax.ppermute(arriving, "chain", to_even))
    pending_rows, _ = backward_levels(arriving)

    forward_pair = jnp.stack([rows[:, :sup_rows] for rows in solved])
    pending_pair = jnp.stack([rows[:, :sup_rows] for rows in pending_rows])
    forward_own = jnp.where(is_odd, forward_pair[levels:], forward_pair[:levels])
    pending_own = jnp.where(is_odd, pending_pair[levels:], pending_pair[:levels])
    answers = jnp.stack(
        [
            paired_matmul(pending_own[level], jnp.concatenate(split_parts(inverse_diag[level, 0], 2), axis=0))
            for level in range(levels)
        ]
    )
    return (forward_own[:, None], answers[:, None])


def solution(mesh):
    return jax.shard_map(
        shards,
        mesh=mesh,
        in_specs=(
            P("chain", "grp", None, None),
            P("chain", "grp", None, None, None),
            P("chain", "grp", None, None),
            P("chain", None, None),
        ),
        out_specs=(P("chain", "grp", None, None), P("chain", "grp", None, None)),
        check_vma=False,
    )
```

```python
import jax
import jax.numpy as jnp
from jax import lax
from jax.sharding import PartitionSpec as P

PRECISE = lax.Precision.HIGHEST


def matmul(left_side, right_factor):
    return jnp.dot(left_side, right_factor, precision=PRECISE, preferred_element_type=jnp.float32)


def matmul_trans(left_side, right_factor):
    return lax.dot_general(
        left_side,
        right_factor,
        (((1,), (1,)), ((), ())),
        precision=PRECISE,
        preferred_element_type=jnp.float32,
    )


TERMS = 3


def split_parts(value, count):
    parts = []
    rest = value
    for _ in range(count):
        part = rest.astype(jnp.bfloat16)
        parts.append(part)
        rest = rest - part.astype(jnp.float32)
    return parts


def term_pairs(count):
    return [(left, right) for left in range(count) for right in range(count) if left + right < count]


def stack_right(value, count):
    parts = split_parts(value, count)
    return jnp.concatenate([parts[right] for _, right in term_pairs(count)], axis=0)


def split_matmul(left_side, stacked):
    count = 2 if TERMS == 3 else 3
    parts = split_parts(left_side, count)
    stacked_left = jnp.concatenate([parts[left] for left, _ in term_pairs(count)], axis=1)
    return jnp.dot(stacked_left, stacked, preferred_element_type=jnp.float32)


def shards(right_side, factor, inverse_diag, pattern):
    levels = right_side.shape[0]
    samples = right_side.shape[2]
    sup_rows = right_side.shape[3]
    groups = lax.axis_size("grp")
    chain = lax.axis_size("chain")
    level_rows = groups * sup_rows
    my_group = lax.axis_index("grp")
    inverse_high, inverse_low = split_parts(inverse_diag, 2)
    factor_high, factor_low = split_parts(factor, 2)
    side_high, side_low = split_parts(right_side, 2)
    scaled = jnp.einsum(
        "lgti,lgkij->lgktj",
        jnp.concatenate([inverse_high, inverse_high, inverse_low], axis=-1),
        jnp.concatenate([factor_high, factor_low, factor_high], axis=-2),
        preferred_element_type=jnp.float32,
    )
    lifted = jnp.einsum(
        "lgsi,lgti->lgst",
        jnp.concatenate([side_high, side_high, side_low], axis=-1),
        jnp.concatenate([inverse_high, inverse_low, inverse_high], axis=-1),
        preferred_element_type=jnp.float32,
    )
    knb = factor.shape[2]
    block_size = knb * sup_rows
    my_chain = lax.axis_index("chain")
    is_odd = my_chain % 2 == 1
    packed = jnp.concatenate(
        [scaled.reshape(levels, block_size, sup_rows), lifted.reshape(levels, samples, sup_rows)], axis=1
    )
    own_pieces = [packed]
    for shift in range(1, groups):
        own_pieces.append(lax.ppermute(packed, "grp", [(h, (h + shift) % groups) for h in range(groups)]))
    partner_pieces = []
    for shift in range(groups):
        pairs = [
            (position * groups + h, (position ^ 1) * groups + (h + shift) % groups)
            for position in range(chain)
            for h in range(groups)
        ]
        partner_pieces.append(lax.ppermute(packed, ("chain", "grp"), pairs))
    swap = [(position, position ^ 1) for position in range(chain)]
    partner_pattern = lax.ppermute(pattern, "chain", swap)
    own_stacked = jnp.stack(own_pieces, axis=1)
    partner_stacked = jnp.stack(partner_pieces, axis=1)
    pair_stacked = jnp.concatenate(
        [jnp.where(is_odd, partner_stacked, own_stacked), jnp.where(is_odd, own_stacked, partner_stacked)], axis=0
    )
    pair_pattern = jnp.concatenate(
        [jnp.where(is_odd, partner_pattern, pattern), jnp.where(is_odd, pattern, partner_pattern)], axis=0
    )
    pair_levels = 2 * levels
    blocks = pair_stacked[:, :, :block_size].reshape(pair_levels, groups, knb, sup_rows, sup_rows)
    offsets = pair_stacked[:, :, block_size:]
    slot_group = (my_group - jnp.arange(groups, dtype=jnp.int32)) % groups
    pattern_slots = jnp.take(pair_pattern, slot_group, axis=1)
    onehot = (pattern_slots[..., None] == slot_group).astype(jnp.float32)
    coupling = jnp.einsum(
        "lgkh,lgktj->lgthj", onehot, blocks, precision=PRECISE, preferred_element_type=jnp.float32
    )
    coupling = coupling.reshape(pair_levels, level_rows, level_rows)
    sources = offsets.transpose(0, 2, 1, 3).reshape(pair_levels, samples, level_rows)

    count = 2 if TERMS == 3 else 3
    chosen_parts = []
    forward_stacks = []
    for level in range(pair_levels):
        chosen_parts.append(split_parts(coupling[level], 2))
        forward_stacks.append(jnp.concatenate(chosen_parts[-1], axis=1))

    def row_stacked(state):
        high, low = split_parts(state, 2)
        return jnp.concatenate(
            [jnp.concatenate([high, high], axis=1), jnp.concatenate([low, jnp.zeros_like(low)], axis=1)], axis=0
        )

    def paired_matmul(state, stacked):
        out = jnp.dot(row_stacked(state), stacked, preferred_element_type=jnp.float32)
        return out[:samples] + out[samples:]

    def forward_product(state, stacked):
        out = lax.dot_general(
            row_stacked(state), stacked, (((1,), (1,)), ((), ())), preferred_element_type=jnp.float32
        )
        return out[:samples] + out[samples:]

    def forward_levels(state, start=0):
        rows = []
        for level in range(start, pair_levels):
            state = sources[level] - forward_product(state, forward_stacks[level])
            rows.append(state)
        return rows

    pair_count = chain // 2
    evens = [(2 * pair, 2 * pair + 2) for pair in range(pair_count - 1)]
    odds = [(2 * pair + 3, 2 * pair + 1) for pair in range(pair_count - 1)]
    to_odd = [(2 * pair, 2 * pair + 1) for pair in range(pair_count)]
    to_even = [(2 * pair + 1, 2 * pair) for pair in range(pair_count)]

    def forward_hop(_, state):
        return lax.ppermute(forward_levels(state)[-1], "chain", evens)

    incoming = jnp.zeros((samples, level_rows), jnp.float32)
    if pair_count > 1:
        first_out = forward_levels(sources[0], 1)[-1] if pair_levels > 1 else sources[0]
        incoming = lax.ppermute(first_out, "chain", evens)
        chosen_parts, _ = lax.optimization_barrier((chosen_parts, first_out))
    backward_stacks = [jnp.concatenate(chosen, axis=0) for chosen in chosen_parts]
    incoming = lax.fori_loop(1, pair_count - 1, forward_hop, incoming, unroll=chain <= 8)
    incoming = jnp.where(is_odd, lax.ppermute(incoming, "chain", to_odd), incoming)
    solved = forward_levels(incoming)

    def backward_levels(running):
        rows = [None] * pair_levels
        for level in reversed(range(pair_levels)):
            rows[level] = solved[level] - running
            running = paired_matmul(rows[level], backward_stacks[level])
        return rows, running

    def backward_hop(_, running):
        return lax.ppermute(backward_levels(running)[1], "chain", odds)

    arriving = jnp.zeros((samples, level_rows), jnp.float32)
    arriving = lax.fori_loop(0, pair_count - 1, backward_hop, arriving, unroll=chain <= 8)
    arriving = jnp.where(is_odd, arriving, lax.ppermute(arriving, "chain", to_even))
    pending_rows, _ = backward_levels(arriving)

    forward_pair = jnp.stack([rows[:, :sup_rows] for rows in solved])
    pending_pair = jnp.stack([rows[:, :sup_rows] for rows in pending_rows])
    forward_own = jnp.where(is_odd, forward_pair[levels:], forward_pair[:levels])
    pending_own = jnp.where(is_odd, pending_pair[levels:], pending_pair[:levels])
    answers = jnp.stack(
        [
            paired_matmul(pending_own[level], jnp.concatenate(split_parts(inverse_diag[level, 0], 2), axis=0))
            for level in range(levels)
        ]
    )
    return (forward_own[:, None], answers[:, None])


def solution(mesh):
    return jax.shard_map(
        shards,
        mesh=mesh,
        in_specs=(
            P("chain", "grp", None, None),
            P("chain", "grp", None, None, None),
            P("chain", "grp", None, None),
            P("chain", None, None),
        ),
        out_specs=(P("chain", "grp", None, None), P("chain", "grp", None, None)),
        check_vma=False,
    )
```

```python
import jax
import jax.numpy as jnp
from jax import lax
from jax.sharding import PartitionSpec as P

PRECISE = lax.Precision.HIGHEST


def matmul(left_side, right_factor):
    return jnp.dot(left_side, right_factor, precision=PRECISE, preferred_element_type=jnp.float32)


def matmul_trans(left_side, right_factor):
    return lax.dot_general(
        left_side,
        right_factor,
        (((1,), (1,)), ((), ())),
        precision=PRECISE,
        preferred_element_type=jnp.float32,
    )


TERMS = 3


def split_parts(value, count):
    parts = []
    rest = value
    for _ in range(count):
        part = rest.astype(jnp.bfloat16)
        parts.append(part)
        rest = rest - part.astype(jnp.float32)
    return parts


def term_pairs(count):
    return [(left, right) for left in range(count) for right in range(count) if left + right < count]


def stack_right(value, count):
    parts = split_parts(value, count)
    return jnp.concatenate([parts[right] for _, right in term_pairs(count)], axis=0)


def split_matmul(left_side, stacked):
    count = 2 if TERMS == 3 else 3
    parts = split_parts(left_side, count)
    stacked_left = jnp.concatenate([parts[left] for left, _ in term_pairs(count)], axis=1)
    return jnp.dot(stacked_left, stacked, preferred_element_type=jnp.float32)


def shards(right_side, factor, inverse_diag, pattern):
    levels = right_side.shape[0]
    samples = right_side.shape[2]
    sup_rows = right_side.shape[3]
    groups = lax.axis_size("grp")
    chain = lax.axis_size("chain")
    level_rows = groups * sup_rows
    my_group = lax.axis_index("grp")
    scaled = jnp.einsum(
        "lgti,lgkij->lgktj",
        inverse_diag,
        factor,
        precision=PRECISE,
        preferred_element_type=jnp.float32,
    )
    lifted = jnp.einsum(
        "lgsi,lgti->lgst",
        right_side,
        inverse_diag,
        precision=PRECISE,
        preferred_element_type=jnp.float32,
    )
    knb = factor.shape[2]
    block_size = knb * sup_rows
    my_chain = lax.axis_index("chain")
    is_odd = my_chain % 2 == 1
    packed = jnp.concatenate(
        [scaled.reshape(levels, block_size, sup_rows), lifted.reshape(levels, samples, sup_rows)], axis=1
    )
    own_pieces = [packed]
    for shift in range(1, groups):
        own_pieces.append(lax.ppermute(packed, "grp", [(h, (h + shift) % groups) for h in range(groups)]))
    partner_pieces = []
    for shift in range(groups):
        pairs = [
            (position * groups + h, (position ^ 1) * groups + (h + shift) % groups)
            for position in range(chain)
            for h in range(groups)
        ]
        partner_pieces.append(lax.ppermute(packed, ("chain", "grp"), pairs))
    swap = [(position, position ^ 1) for position in range(chain)]
    partner_pattern = lax.ppermute(pattern, "chain", swap)
    own_stacked = jnp.stack(own_pieces, axis=1)
    partner_stacked = jnp.stack(partner_pieces, axis=1)
    pair_stacked = jnp.concatenate(
        [jnp.where(is_odd, partner_stacked, own_stacked), jnp.where(is_odd, own_stacked, partner_stacked)], axis=0
    )
    pair_pattern = jnp.concatenate(
        [jnp.where(is_odd, partner_pattern, pattern), jnp.where(is_odd, pattern, partner_pattern)], axis=0
    )
    pair_levels = 2 * levels
    blocks = pair_stacked[:, :, :block_size].reshape(pair_levels, groups, knb, sup_rows, sup_rows)
    offsets = pair_stacked[:, :, block_size:]
    slot_group = (my_group - jnp.arange(groups, dtype=jnp.int32)) % groups
    pattern_slots = jnp.take(pair_pattern, slot_group, axis=1)
    onehot = (pattern_slots[..., None] == slot_group).astype(jnp.float32)
    coupling = jnp.einsum(
        "lgkh,lgktj->lgthj", onehot, blocks, precision=PRECISE, preferred_element_type=jnp.float32
    )
    coupling = coupling.reshape(pair_levels, level_rows, level_rows)
    sources = offsets.transpose(0, 2, 1, 3).reshape(pair_levels, samples, level_rows)

    count = 2 if TERMS == 3 else 3
    chosen_parts = []
    forward_stacks = []
    for level in range(pair_levels):
        chosen_parts.append(split_parts(coupling[level], 2))
        forward_stacks.append(jnp.concatenate([part.T for part in chosen_parts[-1]], axis=0))

    def row_stacked(state):
        high, low = split_parts(state, 2)
        return jnp.concatenate(
            [jnp.concatenate([high, high], axis=1), jnp.concatenate([low, jnp.zeros_like(low)], axis=1)], axis=0
        )

    def paired_matmul(state, stacked):
        out = jnp.dot(row_stacked(state), stacked, preferred_element_type=jnp.float32)
        return out[:samples] + out[samples:]

    def forward_product(state, stacked):
        out = lax.dot_general(
            row_stacked(state), stacked, (((1,), (1,)), ((), ())), preferred_element_type=jnp.float32
        )
        return out[:samples] + out[samples:]

    def forward_levels(state, start=0):
        rows = []
        for level in range(start, pair_levels):
            state = sources[level] - paired_matmul(state, forward_stacks[level])
            rows.append(state)
        return rows

    pair_count = chain // 2
    evens = [(2 * pair, 2 * pair + 2) for pair in range(pair_count - 1)]
    odds = [(2 * pair + 3, 2 * pair + 1) for pair in range(pair_count - 1)]
    to_odd = [(2 * pair, 2 * pair + 1) for pair in range(pair_count)]
    to_even = [(2 * pair + 1, 2 * pair) for pair in range(pair_count)]

    def forward_hop(_, state):
        return lax.ppermute(forward_levels(state)[-1], "chain", evens)

    incoming = jnp.zeros((samples, level_rows), jnp.float32)
    if pair_count > 1:
        first_out = forward_levels(sources[0], 1)[-1] if pair_levels > 1 else sources[0]
        incoming = lax.ppermute(first_out, "chain", evens)
        chosen_parts, _ = lax.optimization_barrier((chosen_parts, first_out))
    backward_stacks = [jnp.concatenate(chosen, axis=0) for chosen in chosen_parts]
    incoming = lax.fori_loop(1, pair_count - 1, forward_hop, incoming, unroll=chain <= 8)
    incoming = jnp.where(is_odd, lax.ppermute(incoming, "chain", to_odd), incoming)
    solved = forward_levels(incoming)

    def backward_levels(running):
        rows = [None] * pair_levels
        for level in reversed(range(pair_levels)):
            rows[level] = solved[level] - running
            running = paired_matmul(rows[level], backward_stacks[level])
        return rows, running

    def backward_hop(_, running):
        return lax.ppermute(backward_levels(running)[1], "chain", odds)

    arriving = jnp.zeros((samples, level_rows), jnp.float32)
    arriving = lax.fori_loop(0, pair_count - 1, backward_hop, arriving, unroll=chain <= 8)
    arriving = jnp.where(is_odd, arriving, lax.ppermute(arriving, "chain", to_even))
    pending_rows, _ = backward_levels(arriving)

    forward_pair = jnp.stack([rows[:, :sup_rows] for rows in solved])
    pending_pair = jnp.stack([rows[:, :sup_rows] for rows in pending_rows])
    forward_own = jnp.where(is_odd, forward_pair[levels:], forward_pair[:levels])
    pending_own = jnp.where(is_odd, pending_pair[levels:], pending_pair[:levels])
    answers = jnp.stack(
        [
            paired_matmul(pending_own[level], jnp.concatenate(split_parts(inverse_diag[level, 0], 2), axis=0))
            for level in range(levels)
        ]
    )
    return (forward_own[:, None], answers[:, None])


def solution(mesh):
    return jax.shard_map(
        shards,
        mesh=mesh,
        in_specs=(
            P("chain", "grp", None, None),
            P("chain", "grp", None, None, None),
            P("chain", "grp", None, None),
            P("chain", None, None),
        ),
        out_specs=(P("chain", "grp", None, None), P("chain", "grp", None, None)),
        check_vma=False,
    )
```
